512 devices in a mesh: cfg: 2 (over y_hi), req: 8 (over y_lo, core), seq: 32 (over z, x).
Axes of the slice: x: 4, y: 8 (y_hi: 2, y_lo: 4; y = y_hi * 4 + y_lo), z: 8, core: 2. Of those that a mesh axis runs over, the one named last changes fastest.
Arguments:
- query: bfloat16 [2, 8, 1024, 768], P('cfg', 'req', 'seq'), may hold values from -6 to 6
- key_value: bfloat16 [2, 2, 8, 1280, 768], P(None, 'cfg', 'req', 'seq'), may hold values from -6 to 6
- residual_in: bfloat16 [2, 8, 1024, 1536], P('cfg', 'req', 'seq'), may hold values from -0.119628906 to 0.119628906
- text_len: int32 [2, 8], P('cfg', 'req'), may hold values from 1 to 154, as said below
- attn_gate: float32 [2, 8, 1536], P('cfg', 'req'), may hold values from 0.5 to 2
- mlp_shift: float32 [2, 8, 1536], P('cfg', 'req'), may hold values from -3 to 3
- mlp_scale: float32 [2, 8, 1536], P('cfg', 'req'), may hold values from -3 to 3
- mlp_gate: float32 [2, 8, 1536], P('cfg', 'req'), may hold values from 0.5 to 2
- shift: float32 [2, 8, 1536], P('cfg', 'req'), may hold values from -3 to 3
- scale: float32 [2, 8, 1536], P('cfg', 'req'), may hold values from -3 to 3
- w_proj: bfloat16 [768, 1536], P(None, 'req'), may hold values from -0.21875 to 0.21875
- w_up: bfloat16 [1536, 3072], P(None, 'req'), may hold values from -0.15625 to 0.15625
- w_down: bfloat16 [3072, 1536], P('req'), may hold values from -0.109375 to 0.109375
- w_out: bfloat16 [1536, 64], replicated, may hold values from -1 to 1
- latent: float32 [8, 1024, 64], P('req', 'seq', 'cfg'), may hold values from -6 to 6
- step_size: float32 [8], P('req'), may hold values from 0.1 to 0.5
Outputs:
- latent_next: float32 [8, 1024, 64], P('req', 'seq', 'cfg')
- guided_norm: float32 [8], P('req')
- peak: float32 [8], P('req')
The draws below stay inside these ranges and needn't reach their ends.
Inputs may be any that keep to these rules, and one draw needn't show every extreme that they name: `text_len`: some entry equals 154.
All inputs are finite; a program needn't handle non-finite values.
Results may differ from the reference program's by a relative error of at most 0.015.
Values may be sent and summed in bfloat16 or wider, within the bound.
No kernel may reach another device: no remote copies, remote signals or barrier semaphores. Data moves between devices by JAX's collectives and lax.ppermute only.
A program may use at most 64 MiB of HBM per device.

```python
import math
import jax
import jax.numpy as jnp
from jax import lax

D = 1536
HEADS = 12
HD = 64
FF = 3072
OUTC = 64
TXT_MAX = 154
IMG_DEV = 32
REQS = 8
IMG = 1024
JOINT = 1280
N_SEQ = 32


def drawn_pair(key):
    width = HEADS * HD
    base_key = jax.random.fold_in(key, 11)
    query_base = jnp.clip(jax.random.normal(jax.random.fold_in(base_key, 1), (2, REQS, IMG, width), jnp.float32), -4.0, 4.0)
    key_base = jnp.clip(jax.random.normal(jax.random.fold_in(base_key, 2), (2, REQS, JOINT, width), jnp.float32), -4.0, 4.0)
    value_base = jnp.clip(jax.random.normal(jax.random.fold_in(base_key, 3), (2, REQS, JOINT, width), jnp.float32), -4.0, 4.0)
    return (query_base, jnp.stack([key_base, value_base]))


def draw_query(key, part):
    query_base, pair_base = drawn_pair(key)
    return query_base.astype(jnp.bfloat16)


def draw_key_value(key, part):
    query_base, pair_base = drawn_pair(key)
    return pair_base.astype(jnp.bfloat16)


def draw_text_len(key, part):
    base_len = jax.random.randint(jax.random.fold_in(key, 21), (2 * REQS,), 1, TXT_MAX + 1)
    chosen_spot = jax.random.randint(jax.random.fold_in(key, 22), (), 0, 2 * REQS)
    flat_len = jnp.where(jnp.arange(2 * REQS, dtype=jnp.int32) == chosen_spot, TXT_MAX, base_len)
    return flat_len.reshape(2, REQS).astype(jnp.int32)


def draw_w_out(key, part):
    out_key = jax.random.fold_in(key, 31)
    column = jnp.arange(OUTC, dtype=jnp.int32).astype(jnp.float32) / (OUTC - 1)
    base = jnp.clip(jax.random.normal(out_key, (D, OUTC), jnp.float32), -4.0, 4.0)
    column_scale = jnp.exp((column - 0.5) * 2.3)
    values = base * column_scale[None, :] * D ** (-0.5)
    return jnp.clip(values, -1.0, 1.0).astype(jnp.bfloat16)


def steps_of(key, dims, cuts, least, largest):
    def one(position, blocks):
        draws = jax.random.uniform(jax.random.fold_in(jax.random.fold_in(key, 6), position), (blocks,), jnp.float32, least / len(cuts), largest / len(cuts))
        return jnp.repeat(jnp.exp(draws), dims[position] // blocks).reshape((-1,) + (1,) * (len(dims) - position - 1))

    factor_of = one(*cuts[0])
    for cut in cuts[1:]:
        factor_of = factor_of * one(*cut)
    return factor_of


def scatter_about(stream_key, dims, scale, bound, split=(), held_as=jnp.bfloat16):
    gain = steps_of(stream_key, dims, split, -0.22, 0.18) if split else 1.0
    array = jax.random.normal(stream_key, dims, jnp.float32) * scale * gain
    return jnp.minimum(jnp.maximum(array, -bound), bound).astype(held_as)


def setup_inputs(seed: int = 0) -> dict:
    streams_of = jax.random.split(jax.random.key(seed), 17)
    query = draw_query(jax.random.fold_in(streams_of[16], 71), 0)
    key_value = draw_key_value(jax.random.fold_in(streams_of[16], 71), 0)
    residual_in = scatter_about(streams_of[2], (2, REQS, IMG, D), 0.02, 0.119628906, ((0, 2), (1, 8), (2, 32)))
    text_len = draw_text_len(jax.random.fold_in(streams_of[16], 71), 0)
    attn_gate = jnp.clip(0.5 + 1.5 * jax.random.uniform(streams_of[4], (2, REQS, D), jnp.float32) ** steps_of(streams_of[4], (2, REQS, D), ((0, 2), (1, 8)), -0.2, 0.2), 0.5, 2.0)
    mlp_shift = scatter_about(streams_of[5], (2, REQS, D), 0.5, 3.0, ((0, 2), (1, 8)), jnp.float32)
    mlp_scale = scatter_about(streams_of[6], (2, REQS, D), 0.5, 3.0, ((0, 2), (1, 8)), jnp.float32)
    mlp_gate = jnp.clip(0.5 + 1.5 * jax.random.uniform(streams_of[7], (2, REQS, D), jnp.float32) ** steps_of(streams_of[7], (2, REQS, D), ((0, 2), (1, 8)), -0.2, 0.2), 0.5, 2.0)
    shift = scatter_about(streams_of[8], (2, REQS, D), 0.5, 3.0, ((0, 2), (1, 8)), jnp.float32)
    scale = scatter_about(streams_of[9], (2, REQS, D), 0.5, 3.0, ((0, 2), (1, 8)), jnp.float32)
    w_proj = scatter_about(streams_of[10], (HEADS * HD, D), (HEADS * HD) ** -0.5, 0.21875, ((1, 8),))
    w_up = scatter_about(streams_of[11], (D, FF), D ** -0.5, 0.15625, ((1, 8),))
    w_down = scatter_about(streams_of[12], (FF, D), FF ** -0.5, 0.109375, ((0, 8),))
    w_out = draw_w_out(jax.random.fold_in(streams_of[16], 71), 0)
    latent = scatter_about(streams_of[14], (REQS, IMG, OUTC), 1.0, 6.0, ((0, 8), (1, 32), (2, 2)), jnp.float32)
    step_size = jnp.clip(jnp.exp(math.log(0.5) - 1.609438 * jax.random.uniform(streams_of[15], (REQS,), jnp.float32) ** steps_of(streams_of[15], (REQS,), ((0, 8),), -0.2, 0.2)), 0.1, 0.5)
    return dict(query=query, key_value=key_value, residual_in=residual_in, text_len=text_len, attn_gate=attn_gate, mlp_shift=mlp_shift, mlp_scale=mlp_scale, mlp_gate=mlp_gate, shift=shift, scale=scale, w_proj=w_proj, w_up=w_up, w_down=w_down, w_out=w_out, latent=latent, step_size=step_size)


guidance_weight = 4.0

def key_usable(joint_rows, length):
    rows_dev = joint_rows // N_SEQ
    positions = jnp.arange(joint_rows, dtype=jnp.int32)
    within = positions % rows_dev
    text_slot = positions // rows_dev * (rows_dev - IMG_DEV) + within - IMG_DEV
    return (within < IMG_DEV) | (text_slot < length)

def modulate_rows(hidden, shift_row, scale_row):
    row_mean = lax.optimization_barrier(jnp.mean(hidden, axis=1, keepdims=True))
    centered = hidden - row_mean
    row_var = lax.optimization_barrier(jnp.mean(centered * centered, axis=1, keepdims=True))
    return (centered * lax.rsqrt(row_var + 1e-06) * (1.0 + scale_row[None, :]) + shift_row[None, :]).astype(jnp.bfloat16)

def half_layer(query_rows, key_rows, value_rows, residual_rows, length, gate_row, mshift_row, mscale_row, mgate_row, shift_row, scale_row, w_proj, w_up, w_down, w_out):
    image_rows = query_rows.shape[0]
    joint_rows = key_rows.shape[0]
    usable = key_usable(joint_rows, length)
    query_heads = query_rows.reshape(image_rows, HEADS, HD).transpose(1, 0, 2)
    key_heads = key_rows.reshape(joint_rows, HEADS, HD).transpose(1, 0, 2)
    value_heads = value_rows.reshape(joint_rows, HEADS, HD).transpose(1, 0, 2)

    def one_head(parts):
        query_head, key_head, value_head = parts
        logits = jnp.dot(query_head, key_head.T, preferred_element_type=jnp.float32) * HD ** (-0.5)
        row_max = lax.optimization_barrier(jnp.max(jnp.where(usable[None, :], logits, -1e+30), axis=1, keepdims=True))
        weights = jnp.where(usable[None, :], jnp.exp(logits - row_max), 0.0)
        denominator = lax.optimization_barrier(jnp.sum(weights, axis=1, keepdims=True))
        return jnp.dot(weights.astype(jnp.bfloat16), value_head, preferred_element_type=jnp.float32) / denominator
    head_out = lax.map(one_head, (query_heads, key_heads, value_heads))
    attended = head_out.transpose(1, 0, 2).reshape(image_rows, HEADS * HD).astype(jnp.bfloat16)
    projected = jnp.dot(attended, w_proj, preferred_element_type=jnp.float32)
    hidden = residual_rows.astype(jnp.float32) + gate_row[None, :] * projected
    mlp_in = modulate_rows(hidden, mshift_row, mscale_row)
    inner = jax.nn.gelu(jnp.dot(mlp_in, w_up, preferred_element_type=jnp.float32), approximate=True).astype(jnp.bfloat16)
    mlp_out = jnp.dot(inner, w_down, preferred_element_type=jnp.float32)
    hidden_two = hidden + mgate_row[None, :] * mlp_out
    modulated = modulate_rows(hidden_two, shift_row, scale_row)
    return jnp.dot(modulated, w_out, preferred_element_type=jnp.float32)

def reference(query, key_value, residual_in, text_len, attn_gate, mlp_shift, mlp_scale, mlp_gate, shift, scale, w_proj, w_up, w_down, w_out, latent, step_size):
    width = HEADS * HD
    flat_query = query.reshape(2 * REQS, IMG, width)
    flat_keys = key_value[0].reshape(2 * REQS, JOINT, width)
    flat_values = key_value[1].reshape(2 * REQS, JOINT, width)
    flat_resid = residual_in.reshape(2 * REQS, IMG, D)
    flat_len = text_len.reshape(2 * REQS).astype(jnp.int32)
    flat_gate = attn_gate.reshape(2 * REQS, D)
    flat_mshift = mlp_shift.reshape(2 * REQS, D)
    flat_mscale = mlp_scale.reshape(2 * REQS, D)
    flat_mgate = mlp_gate.reshape(2 * REQS, D)
    flat_shift = shift.reshape(2 * REQS, D)
    flat_scale = scale.reshape(2 * REQS, D)

    def one_pair(parts):
        return half_layer(parts[0], parts[1], parts[2], parts[3], parts[4], parts[5], parts[6], parts[7], parts[8], parts[9], parts[10], w_proj, w_up, w_down, w_out)
    velocity = lax.map(one_pair, (flat_query, flat_keys, flat_values, flat_resid, flat_len, flat_gate, flat_mshift, flat_mscale, flat_mgate, flat_shift, flat_scale))
    velocity = velocity.reshape(2, REQS, IMG, OUTC)
    cond_part = velocity[0]
    uncond = velocity[1]
    guided = uncond + guidance_weight * (cond_part - uncond)
    entries = IMG * OUTC
    guided_norm = jnp.sqrt(lax.optimization_barrier(jnp.sum(guided * guided, axis=(1, 2))) / entries + 1e-06)
    peak = lax.optimization_barrier(jnp.max(jnp.abs(guided), axis=(1, 2)))
    latent_next = latent + step_size[:, None, None] * guided
    return (latent_next, guided_norm, peak)
```

```python
import jax
import jax.numpy as jnp
from jax import lax
from jax.sharding import PartitionSpec as P

HEADS = 12
HD = 64


guidance_weight = 4.0


def swapped(block, axis, apart):
    count = lax.axis_size(axis)
    route = []
    for low in range(count):
        high = low | 1 << apart
        if high != low and high < count:
            route += [(low, high), (high, low)]
    return lax.ppermute(block, axis, route)


def modulate_rows(hidden, shift_row, scale_row):
    row_mean = jnp.mean(hidden, axis=1, keepdims=True)
    centered = hidden - row_mean
    row_var = jnp.mean(centered * centered, axis=1, keepdims=True)
    return (
        centered * lax.rsqrt(row_var + 1e-06) * (1.0 + scale_row[None, :]) + shift_row[None, :]
    ).astype(jnp.bfloat16)


def per_device(
    query,
    key_value,
    residual_in,
    text_len,
    attn_gate,
    mlp_shift,
    mlp_scale,
    mlp_gate,
    shift,
    scale,
    w_proj,
    w_up,
    w_down,
    w_out,
    latent,
    step_size,
):
    img_dev = query.shape[2]
    rows_dev = key_value.shape[3]
    txt_dev = rows_dev - img_dev
    length = text_len[0, 0]
    queries = query[0, 0].reshape(img_dev, HEADS, HD)
    key_vals = key_value[:, 0, 0]
    factor = HD ** (-0.5)
    piece = lax.all_gather(key_vals, "seq", axis=1, tiled=True)
    running_max = jnp.full((img_dev, HEADS), -1e30, jnp.float32)
    piece_rows = piece.shape[1]
    positions = jnp.arange(piece_rows, dtype=jnp.int32)
    within = positions % rows_dev
    text_slot = positions // rows_dev * txt_dev + within - img_dev
    usable = ((within < img_dev) | (text_slot < length))[None, None, :]
    keys_here = piece[0].reshape(piece_rows, HEADS, HD)
    vals_here = piece[1].reshape(piece_rows, HEADS, HD)
    logits = (
        jnp.einsum("qhd,khd->qhk", queries, keys_here, preferred_element_type=jnp.float32) * factor
    )
    new_max = jnp.maximum(running_max, jnp.max(jnp.where(usable, logits, -1e30), axis=2))
    weights = jnp.where(usable, jnp.exp(logits - new_max[:, :, None]), 0.0)
    running_sum = jnp.sum(weights, axis=2)
    weighted = jnp.einsum(
        "qhk,khd->qhd", weights.astype(jnp.bfloat16), vals_here, preferred_element_type=jnp.float32
    )
    attended = (
        (weighted / running_sum[:, :, None]).reshape(img_dev, HEADS * HD).astype(jnp.bfloat16)
    )
    projected = jnp.dot(
        attended,
        lax.all_gather(w_proj, "req", axis=1, tiled=True),
        preferred_element_type=jnp.float32,
    )
    hidden = residual_in[0, 0].astype(jnp.float32) + attn_gate[0, 0][None, :] * projected
    mlp_in = modulate_rows(hidden, mlp_shift[0, 0], mlp_scale[0, 0])
    inner = jax.nn.gelu(
        jnp.dot(
            lax.all_gather(mlp_in, "req", axis=0, tiled=True),
            w_up,
            preferred_element_type=jnp.float32,
        ),
        approximate=True,
    ).astype(jnp.bfloat16)
    mlp_out = lax.psum_scatter(
        jnp.dot(inner, w_down, preferred_element_type=jnp.float32).astype(jnp.bfloat16),
        "req",
        scatter_dimension=0,
        tiled=True,
    ).astype(jnp.float32)
    hidden_two = hidden + mlp_gate[0, 0][None, :] * mlp_out
    modulated = modulate_rows(hidden_two, shift[0, 0], scale[0, 0])
    velocity = jnp.dot(modulated, w_out, preferred_element_type=jnp.float32)
    half_width = velocity.shape[1] // lax.axis_size("cfg")
    side_index = lax.axis_index("cfg")
    received = swapped(velocity, "cfg", 0)
    is_cond = side_index == 0
    cond_part = jnp.where(is_cond, velocity, received)
    uncond = jnp.where(is_cond, received, velocity)
    guided_full = uncond + guidance_weight * (cond_part - uncond)
    partials = jnp.stack([jnp.sum(guided_full * guided_full), jnp.max(jnp.abs(guided_full))])
    n_seq = lax.axis_size("seq")
    gathered = lax.all_to_all(
        jnp.broadcast_to(partials[None], (n_seq, 2)), "seq", 0, 0, tiled=True
    )
    guided_total = jnp.sum(gathered[:, 0])
    peak_value = jnp.max(gathered[:, 1])
    entries = img_dev * n_seq * velocity.shape[1]
    guided_norm = jnp.sqrt(guided_total / entries + 1e-06)
    guided = lax.dynamic_slice_in_dim(guided_full, side_index * half_width, half_width, 1)
    latent_next = latent + step_size[0] * guided[None, :, :]
    return (latent_next, jnp.reshape(guided_norm, (1,)), jnp.reshape(peak_value, (1,)))


def solution(mesh):
    in_specs = (
        P("cfg", "req", "seq", None),
        P(None, "cfg", "req", "seq", None),
        P("cfg", "req", "seq", None),
        P("cfg", "req"),
        P("cfg", "req", None),
        P("cfg", "req", None),
        P("cfg", "req", None),
        P("cfg", "req", None),
        P("cfg", "req", None),
        P("cfg", "req", None),
        P(None, "req"),
        P(None, "req"),
        P("req", None),
        P(),
        P("req", "seq", "cfg"),
        P("req"),
    )
    out_specs = (P("req", "seq", "cfg"), P("req"), P("req"))
    return jax.shard_map(
        per_device, mesh=mesh, in_specs=in_specs, out_specs=out_specs, check_vma=False
    )
```

```python
import jax
import jax.numpy as jnp
from jax import lax
from jax.sharding import PartitionSpec as P

HEADS = 12
HD = 64


guidance_weight = 4.0


def swapped(block, axis, apart):
    count = lax.axis_size(axis)
    route = []
    for low in range(count):
        high = low | 1 << apart
        if high != low and high < count:
            route += [(low, high), (high, low)]
    return lax.ppermute(block, axis, route)


def modulate_rows(hidden, shift_row, scale_row):
    row_mean = jnp.mean(hidden, axis=1, keepdims=True)
    centered = hidden - row_mean
    row_var = jnp.mean(centered * centered, axis=1, keepdims=True)
    return (
        centered * lax.rsqrt(row_var + 1e-06) * (1.0 + scale_row[None, :]) + shift_row[None, :]
    ).astype(jnp.bfloat16)


def per_device(
    query,
    key_value,
    residual_in,
    text_len,
    attn_gate,
    mlp_shift,
    mlp_scale,
    mlp_gate,
    shift,
    scale,
    w_proj,
    w_up,
    w_down,
    w_out,
    latent,
    step_size,
):
    img_dev = query.shape[2]
    rows_dev = key_value.shape[3]
    txt_dev = rows_dev - img_dev
    length = text_len[0, 0]
    queries = query[0, 0].reshape(img_dev, HEADS, HD)
    key_vals = key_value[:, 0, 0]
    factor = HD ** (-0.5)
    piece = lax.all_gather(key_vals, "seq", axis=1, tiled=True)
    running_max = jnp.full((img_dev, HEADS), -1e30, jnp.float32)
    piece_rows = piece.shape[1]
    positions = jnp.arange(piece_rows, dtype=jnp.int32)
    within = positions % rows_dev
    text_slot = positions // rows_dev * txt_dev + within - img_dev
    usable = ((within < img_dev) | (text_slot < length))[None, None, :]
    keys_here = piece[0].reshape(piece_rows, HEADS, HD)
    vals_here = piece[1].reshape(piece_rows, HEADS, HD)
    logits = (
        jnp.einsum("qhd,khd->qhk", queries, keys_here, preferred_element_type=jnp.float32) * factor
    )
    new_max = jnp.maximum(running_max, jnp.max(jnp.where(usable, logits, -1e30), axis=2))
    weights = jnp.where(usable, jnp.exp(logits - new_max[:, :, None]), 0.0)
    running_sum = jnp.sum(weights, axis=2)
    weighted = jnp.einsum(
        "qhk,khd->qhd", weights.astype(jnp.bfloat16), vals_here, preferred_element_type=jnp.float32
    )
    attended = (
        (weighted / running_sum[:, :, None]).reshape(img_dev, HEADS * HD).astype(jnp.bfloat16)
    )
    n_req = lax.axis_size("req")
    proj_blocks = lax.all_to_all(
        jnp.broadcast_to(w_proj[None], (n_req,) + w_proj.shape), "req", 0, 0, tiled=True
    )
    projected = jnp.einsum(
        "tk,ikc->tic", attended, proj_blocks, preferred_element_type=jnp.float32
    ).reshape(img_dev, n_req * w_proj.shape[1])
    hidden = residual_in[0, 0].astype(jnp.float32) + attn_gate[0, 0][None, :] * projected
    mlp_in = modulate_rows(hidden, mlp_shift[0, 0], mlp_scale[0, 0])
    inner = jax.nn.gelu(
        jnp.dot(
            lax.all_gather(mlp_in, "req", axis=0, tiled=True),
            w_up,
            preferred_element_type=jnp.float32,
        ),
        approximate=True,
    ).astype(jnp.bfloat16)
    mlp_parts = (
        jnp.dot(inner, w_down, preferred_element_type=jnp.float32)
        .astype(jnp.bfloat16)
        .reshape(n_req, img_dev, w_down.shape[1])
    )
    mlp_out = jnp.sum(
        lax.all_to_all(mlp_parts, "req", 0, 0, tiled=True).astype(jnp.float32), axis=0
    )
    hidden_two = hidden + mlp_gate[0, 0][None, :] * mlp_out
    modulated = modulate_rows(hidden_two, shift[0, 0], scale[0, 0])
    velocity = jnp.dot(modulated, w_out, preferred_element_type=jnp.float32)
    half_width = velocity.shape[1] // lax.axis_size("cfg")
    side_index = lax.axis_index("cfg")
    received = swapped(velocity, "cfg", 0)
    is_cond = side_index == 0
    cond_part = jnp.where(is_cond, velocity, received)
    uncond = jnp.where(is_cond, received, velocity)
    guided_full = uncond + guidance_weight * (cond_part - uncond)
    partials = jnp.stack([jnp.sum(guided_full * guided_full), jnp.max(jnp.abs(guided_full))])
    n_seq = lax.axis_size("seq")
    gathered = lax.all_to_all(
        jnp.broadcast_to(partials[None], (n_seq, 2)), "seq", 0, 0, tiled=True
    )
    guided_total = jnp.sum(gathered[:, 0])
    peak_value = jnp.max(gathered[:, 1])
    entries = img_dev * n_seq * velocity.shape[1]
    guided_norm = jnp.sqrt(guided_total / entries + 1e-06)
    guided = lax.dynamic_slice_in_dim(guided_full, side_index * half_width, half_width, 1)
    latent_next = latent + step_size[0] * guided[None, :, :]
    return (latent_next, jnp.reshape(guided_norm, (1,)), jnp.reshape(peak_value, (1,)))


def solution(mesh):
    in_specs = (
        P("cfg", "req", "seq", None),
        P(None, "cfg", "req", "seq", None),
        P("cfg", "req", "seq", None),
        P("cfg", "req"),
        P("cfg", "req", None),
        P("cfg", "req", None),
        P("cfg", "req", None),
        P("cfg", "req", None),
        P("cfg", "req", None),
        P("cfg", "req", None),
        P(None, "req"),
        P(None, "req"),
        P("req", None),
        P(),
        P("req", "seq", "cfg"),
        P("req"),
    )
    out_specs = (P("req", "seq", "cfg"), P("req"), P("req"))
    return jax.shard_map(
        per_device, mesh=mesh, in_specs=in_specs, out_specs=out_specs, check_vma=False
    )
```

```python
import jax
import jax.numpy as jnp
from jax import lax
from jax.sharding import Mesh, PartitionSpec as P

HEADS = 12
HD = 64
SEQ_MINOR = 4


guidance_weight = 4.0


def swapped(block, axis, apart):
    count = lax.axis_size(axis)
    route = []
    for low in range(count):
        high = low | 1 << apart
        if high != low and high < count:
            route += [(low, high), (high, low)]
    return lax.ppermute(block, axis, route)


def modulate_rows(hidden, shift_row, scale_row):
    row_mean = jnp.mean(hidden, axis=1, keepdims=True)
    centered = hidden - row_mean
    row_var = jnp.mean(centered * centered, axis=1, keepdims=True)
    return (
        centered * lax.rsqrt(row_var + 1e-06) * (1.0 + scale_row[None, :]) + shift_row[None, :]
    ).astype(jnp.bfloat16)


def per_device(
    query,
    key_value,
    residual_in,
    text_len,
    attn_gate,
    mlp_shift,
    mlp_scale,
    mlp_gate,
    shift,
    scale,
    w_proj,
    w_up,
    w_down,
    w_out,
    latent,
    step_size,
):
    img_dev = query.shape[2]
    rows_dev = key_value.shape[3]
    txt_dev = rows_dev - img_dev
    length = text_len[0, 0]
    factor = HD ** (-0.5)
    n_x = lax.axis_size("sx")
    x_index = lax.axis_index("sx")
    query_rows = lax.all_gather(query[0, 0], "sx", axis=0, tiled=True)
    piece = lax.all_gather(key_value[:, 0, 0], "sz", axis=1, tiled=True)
    q_rows = query_rows.shape[0]
    piece_rows = piece.shape[1]
    positions = jnp.arange(piece_rows, dtype=jnp.int32)
    within = positions % rows_dev
    source = (positions // rows_dev) * n_x + x_index
    text_slot = source * txt_dev + within - img_dev
    usable = ((within < img_dev) | (text_slot < length))[None, None, :]
    queries = query_rows.reshape(q_rows, HEADS, HD)
    keys_here = piece[0].reshape(piece_rows, HEADS, HD)
    vals_here = piece[1].reshape(piece_rows, HEADS, HD)
    logits = (
        jnp.einsum("qhd,khd->qhk", queries, keys_here, preferred_element_type=jnp.float32) * factor
    )
    part_max = jnp.max(jnp.where(usable, logits, -1e30), axis=2)
    weights = jnp.where(usable, jnp.exp(logits - part_max[:, :, None]), 0.0)
    part_sum = jnp.sum(weights, axis=2)
    weighted = jnp.einsum(
        "qhk,khd->qhd", weights.astype(jnp.bfloat16), vals_here, preferred_element_type=jnp.float32
    )
    width = HEADS * HD
    packed = jnp.concatenate(
        [weighted.reshape(q_rows, width), part_max, part_sum], axis=1
    ).reshape(n_x, img_dev, width + 2 * HEADS)
    got = lax.all_to_all(packed, "sx", 0, 0, tiled=True)
    got_out = got[:, :, :width].reshape(n_x, img_dev, HEADS, HD)
    got_max = got[:, :, width : width + HEADS]
    got_sum = got[:, :, width + HEADS :]
    row_max = jnp.max(got_max, axis=0)
    rescale = jnp.exp(got_max - row_max[None])
    numerator = jnp.sum(rescale[:, :, :, None] * got_out, axis=0)
    denominator = jnp.sum(rescale * got_sum, axis=0)
    attended = (numerator / denominator[:, :, None]).reshape(img_dev, width).astype(jnp.bfloat16)
    n_req = lax.axis_size("req")
    projected = jnp.dot(
        attended,
        lax.all_gather(w_proj, "req", axis=1, tiled=True),
        preferred_element_type=jnp.float32,
    )
    hidden = residual_in[0, 0].astype(jnp.float32) + attn_gate[0, 0][None, :] * projected
    mlp_in = modulate_rows(hidden, mlp_shift[0, 0], mlp_scale[0, 0])
    inner = jax.nn.gelu(
        jnp.dot(
            lax.all_gather(mlp_in, "req", axis=0, tiled=True),
            w_up,
            preferred_element_type=jnp.float32,
        ),
        approximate=True,
    ).astype(jnp.bfloat16)
    mlp_parts = (
        jnp.dot(inner, w_down, preferred_element_type=jnp.float32)
        .astype(jnp.bfloat16)
        .reshape(n_req, img_dev, w_down.shape[1])
    )
    mlp_out = jnp.sum(
        lax.all_to_all(mlp_parts, "req", 0, 0, tiled=True).astype(jnp.float32), axis=0
    )
    hidden_two = hidden + mlp_gate[0, 0][None, :] * mlp_out
    modulated = modulate_rows(hidden_two, shift[0, 0], scale[0, 0])
    velocity = jnp.dot(modulated, w_out, preferred_element_type=jnp.float32)
    half_width = velocity.shape[1] // lax.axis_size("cfg")
    side_index = lax.axis_index("cfg")
    received = swapped(velocity, "cfg", 0)
    is_cond = side_index == 0
    cond_part = jnp.where(is_cond, velocity, received)
    uncond = jnp.where(is_cond, received, velocity)
    guided_full = uncond + guidance_weight * (cond_part - uncond)
    partials = jnp.stack([jnp.sum(guided_full * guided_full), jnp.max(jnp.abs(guided_full))])
    n_seq = lax.axis_size(("sz", "sx"))
    gathered = lax.all_to_all(
        jnp.broadcast_to(partials[None], (n_seq, 2)), ("sz", "sx"), 0, 0, tiled=True
    )
    guided_total = jnp.sum(gathered[:, 0])
    peak_value = jnp.max(gathered[:, 1])
    entries = img_dev * n_seq * velocity.shape[1]
    guided_norm = jnp.sqrt(guided_total / entries + 1e-06)
    guided = lax.dynamic_slice_in_dim(guided_full, side_index * half_width, half_width, 1)
    latent_next = latent + step_size[0] * guided[None, :, :]
    return (latent_next, jnp.reshape(guided_norm, (1,)), jnp.reshape(peak_value, (1,)))


def solution(mesh):
    n_seq = mesh.shape["seq"]
    n_x = SEQ_MINOR if n_seq % SEQ_MINOR == 0 else 1
    split_mesh = Mesh(
        mesh.devices.reshape(mesh.shape["cfg"], mesh.shape["req"], n_seq // n_x, n_x),
        ("cfg", "req", "sz", "sx"),
    )
    seq = ("sz", "sx")
    in_specs = (
        P("cfg", "req", seq, None),
        P(None, "cfg", "req", seq, None),
        P("cfg", "req", seq, None),
        P("cfg", "req"),
        P("cfg", "req", None),
        P("cfg", "req", None),
        P("cfg", "req", None),
        P("cfg", "req", None),
        P("cfg", "req", None),
        P("cfg", "req", None),
        P(None, "req"),
        P(None, "req"),
        P("req", None),
        P(),
        P("req", seq, "cfg"),
        P("req"),
    )
    out_specs = (P("req", seq, "cfg"), P("req"), P("req"))
    return jax.shard_map(
        per_device, mesh=split_mesh, in_specs=in_specs, out_specs=out_specs, check_vma=False
    )
```

```python
import jax
import jax.numpy as jnp
from jax import lax
from jax.sharding import Mesh, PartitionSpec as P

HEADS = 12
HD = 64
SEQ_MINOR = 4
CORES = 2


guidance_weight = 4.0


def swapped(block, axis, apart):
    count = lax.axis_size(axis)
    route = []
    for low in range(count):
        high = low | 1 << apart
        if high != low and high < count:
            route += [(low, high), (high, low)]
    return lax.ppermute(block, axis, route)


def modulate_rows(hidden, shift_row, scale_row):
    row_mean = jnp.mean(hidden, axis=1, keepdims=True)
    centered = hidden - row_mean
    row_var = jnp.mean(centered * centered, axis=1, keepdims=True)
    return (
        centered * lax.rsqrt(row_var + 1e-06) * (1.0 + scale_row[None, :]) + shift_row[None, :]
    ).astype(jnp.bfloat16)


def per_device(
    query,
    key_value,
    residual_in,
    text_len,
    attn_gate,
    mlp_shift,
    mlp_scale,
    mlp_gate,
    shift,
    scale,
    w_proj,
    w_up,
    w_down,
    w_out,
    latent,
    step_size,
):
    img_dev = query.shape[2]
    rows_dev = key_value.shape[3]
    txt_dev = rows_dev - img_dev
    length = text_len[0, 0]
    factor = HD ** (-0.5)
    n_x = lax.axis_size("sx")
    x_index = lax.axis_index("sx")
    query_rows = lax.all_to_all(
        jnp.broadcast_to(query[0, 0][None], (n_x,) + query.shape[2:]), "sx", 0, 0, tiled=True
    ).reshape(n_x * img_dev, query.shape[3])
    piece = lax.all_gather(key_value[:, 0, 0], "sz", axis=1, tiled=True)
    q_rows = query_rows.shape[0]
    piece_rows = piece.shape[1]
    positions = jnp.arange(piece_rows, dtype=jnp.int32)
    within = positions % rows_dev
    source = (positions // rows_dev) * n_x + x_index
    text_slot = source * txt_dev + within - img_dev
    usable = ((within < img_dev) | (text_slot < length))[None, None, :]
    queries = query_rows.reshape(q_rows, HEADS, HD)
    keys_here = piece[0].reshape(piece_rows, HEADS, HD)
    vals_here = piece[1].reshape(piece_rows, HEADS, HD)
    logits = (
        jnp.einsum("qhd,khd->qhk", queries, keys_here, preferred_element_type=jnp.float32) * factor
    )
    part_max = jnp.max(jnp.where(usable, logits, -1e30), axis=2)
    weights = jnp.where(usable, jnp.exp(logits - part_max[:, :, None]), 0.0)
    part_sum = jnp.sum(weights, axis=2)
    weighted = jnp.einsum(
        "qhk,khd->qhd", weights.astype(jnp.bfloat16), vals_here, preferred_element_type=jnp.float32
    )
    width = HEADS * HD
    packed = jnp.concatenate(
        [weighted.reshape(q_rows, width), part_max, part_sum], axis=1
    ).reshape(n_x, img_dev, width + 2 * HEADS)
    got = lax.all_to_all(packed, "sx", 0, 0, tiled=True)
    got_out = got[:, :, :width].reshape(n_x, img_dev, HEADS, HD)
    got_max = got[:, :, width : width + HEADS]
    got_sum = got[:, :, width + HEADS :]
    row_max = jnp.max(got_max, axis=0)
    rescale = jnp.exp(got_max - row_max[None])
    numerator = jnp.sum(rescale[:, :, :, None] * got_out, axis=0)
    denominator = jnp.sum(rescale * got_sum, axis=0)
    attended = (numerator / denominator[:, :, None]).reshape(img_dev, width).astype(jnp.bfloat16)
    projected = jnp.dot(
        attended,
        lax.all_gather(w_proj, ("ry", "rc"), axis=1, tiled=True),
        preferred_element_type=jnp.float32,
    )
    hidden = residual_in[0, 0].astype(jnp.float32) + attn_gate[0, 0][None, :] * projected
    mlp_in = modulate_rows(hidden, mlp_shift[0, 0], mlp_scale[0, 0])
    n_y = lax.axis_size("ry")
    pair = [(0, 1), (1, 0)]
    up_other = lax.ppermute(w_up, "rc", pair)
    down_other = lax.ppermute(w_down, "rc", pair)
    line_in = lax.all_gather(mlp_in, "ry", axis=0, tiled=True)
    inner_own = jax.nn.gelu(
        jnp.dot(line_in, w_up, preferred_element_type=jnp.float32), approximate=True
    ).astype(jnp.bfloat16)
    inner_other = jax.nn.gelu(
        jnp.dot(line_in, up_other, preferred_element_type=jnp.float32), approximate=True
    ).astype(jnp.bfloat16)
    mlp_parts = (
        (
            jnp.dot(inner_own, w_down, preferred_element_type=jnp.float32)
            + jnp.dot(inner_other, down_other, preferred_element_type=jnp.float32)
        )
        .astype(jnp.bfloat16)
        .reshape(n_y, img_dev, w_down.shape[1])
    )
    mlp_out = jnp.sum(
        lax.all_to_all(mlp_parts, "ry", 0, 0, tiled=True).astype(jnp.float32), axis=0
    )
    hidden_two = hidden + mlp_gate[0, 0][None, :] * mlp_out
    modulated = modulate_rows(hidden_two, shift[0, 0], scale[0, 0])
    velocity = jnp.dot(modulated, w_out, preferred_element_type=jnp.float32)
    half_width = velocity.shape[1] // lax.axis_size("cfg")
    side_index = lax.axis_index("cfg")
    received = swapped(velocity, "cfg", 0)
    is_cond = side_index == 0
    cond_part = jnp.where(is_cond, velocity, received)
    uncond = jnp.where(is_cond, received, velocity)
    guided_full = uncond + guidance_weight * (cond_part - uncond)
    partials = jnp.stack([jnp.sum(guided_full * guided_full), jnp.max(jnp.abs(guided_full))])
    n_seq = lax.axis_size(("sz", "sx"))
    gathered = lax.all_to_all(
        jnp.broadcast_to(partials[None], (n_seq, 2)), ("sz", "sx"), 0, 0, tiled=True
    )
    guided_total = jnp.sum(gathered[:, 0])
    peak_value = jnp.max(gathered[:, 1])
    entries = img_dev * n_seq * velocity.shape[1]
    guided_norm = jnp.sqrt(guided_total / entries + 1e-06)
    guided = lax.dynamic_slice_in_dim(guided_full, side_index * half_width, half_width, 1)
    latent_next = latent + step_size[0] * guided[None, :, :]
    return (latent_next, jnp.reshape(guided_norm, (1,)), jnp.reshape(peak_value, (1,)))


def solution(mesh):
    n_seq = mesh.shape["seq"]
    n_req = mesh.shape["req"]
    n_x = SEQ_MINOR if n_seq % SEQ_MINOR == 0 else 1
    n_core = CORES if n_req % CORES == 0 else 1
    split_mesh = Mesh(
        mesh.devices.reshape(mesh.shape["cfg"], n_req // n_core, n_core, n_seq // n_x, n_x),
        ("cfg", "ry", "rc", "sz", "sx"),
    )
    req = ("ry", "rc")
    seq = ("sz", "sx")
    in_specs = (
        P("cfg", req, seq, None),
        P(None, "cfg", req, seq, None),
        P("cfg", req, seq, None),
        P("cfg", req),
        P("cfg", req, None),
        P("cfg", req, None),
        P("cfg", req, None),
        P("cfg", req, None),
        P("cfg", req, None),
        P("cfg", req, None),
        P(None, req),
        P(None, req),
        P(req, None),
        P(),
        P(req, seq, "cfg"),
        P(req),
    )
    out_specs = (P(req, seq, "cfg"), P(req), P(req))
    return jax.shard_map(
        per_device, mesh=split_mesh, in_specs=in_specs, out_specs=out_specs, check_vma=False
    )
```

```python
import jax
import jax.numpy as jnp
from jax import lax
from jax.sharding import Mesh, PartitionSpec as P

HEADS = 12
HD = 64
SEQ_MINOR = 4
CORES = 2


guidance_weight = 4.0


def swapped(block, axis, apart):
    count = lax.axis_size(axis)
    route = []
    for low in range(count):
        high = low | 1 << apart
        if high != low and high < count:
            route += [(low, high), (high, low)]
    return lax.ppermute(block, axis, route)


def modulate_rows(hidden, shift_row, scale_row):
    row_mean = jnp.mean(hidden, axis=1, keepdims=True)
    centered = hidden - row_mean
    row_var = jnp.mean(centered * centered, axis=1, keepdims=True)
    return (
        centered * lax.rsqrt(row_var + 1e-06) * (1.0 + scale_row[None, :]) + shift_row[None, :]
    ).astype(jnp.bfloat16)


def per_device(
    query,
    key_value,
    residual_in,
    text_len,
    attn_gate,
    mlp_shift,
    mlp_scale,
    mlp_gate,
    shift,
    scale,
    w_proj,
    w_up,
    w_down,
    w_out,
    latent,
    step_size,
):
    img_dev = query.shape[2]
    rows_dev = key_value.shape[3]
    txt_dev = rows_dev - img_dev
    length = text_len[0, 0]
    factor = HD ** (-0.5)
    n_x = lax.axis_size("sx")
    x_index = lax.axis_index("sx")
    query_rows = lax.all_to_all(
        jnp.broadcast_to(query[0, 0][None], (n_x,) + query.shape[2:]), "sx", 0, 0, tiled=True
    ).reshape(n_x * img_dev, query.shape[3])
    piece = lax.all_gather(key_value[:, 0, 0], "sz", axis=1, tiled=True)
    q_rows = query_rows.shape[0]
    piece_rows = piece.shape[1]
    positions = jnp.arange(piece_rows, dtype=jnp.int32)
    within = positions % rows_dev
    source = (positions // rows_dev) * n_x + x_index
    text_slot = source * txt_dev + within - img_dev
    usable = ((within < img_dev) | (text_slot < length))[None, None, :]
    queries = query_rows.reshape(q_rows, HEADS, HD)
    keys_here = piece[0].reshape(piece_rows, HEADS, HD)
    vals_here = piece[1].reshape(piece_rows, HEADS, HD)
    logits = (
        jnp.einsum("qhd,khd->qhk", queries, keys_here, preferred_element_type=jnp.float32) * factor
    )
    part_max = jnp.max(jnp.where(usable, logits, -1e30), axis=2)
    weights = jnp.where(usable, jnp.exp(logits - part_max[:, :, None]), 0.0)
    part_sum = jnp.sum(weights, axis=2)
    weighted = jnp.einsum(
        "qhk,khd->qhd", weights.astype(jnp.bfloat16), vals_here, preferred_element_type=jnp.float32
    )
    width = HEADS * HD
    packed = jnp.concatenate(
        [weighted.reshape(q_rows, width), part_max, part_sum], axis=1
    ).reshape(n_x, img_dev, width + 2 * HEADS)
    got = lax.all_to_all(packed, "sx", 0, 0, tiled=True)
    got_out = got[:, :, :width].reshape(n_x, img_dev, HEADS, HD)
    got_max = got[:, :, width : width + HEADS]
    got_sum = got[:, :, width + HEADS :]
    row_max = jnp.max(got_max, axis=0)
    rescale = jnp.exp(got_max - row_max[None])
    numerator = jnp.sum(rescale[:, :, :, None] * got_out, axis=0)
    denominator = jnp.sum(rescale * got_sum, axis=0)
    attended = (numerator / denominator[:, :, None]).reshape(img_dev, width).astype(jnp.bfloat16)
    projected = jnp.dot(
        attended,
        lax.all_gather(w_proj, ("ry", "rc"), axis=1, tiled=True),
        preferred_element_type=jnp.float32,
    )
    hidden = residual_in[0, 0].astype(jnp.float32) + attn_gate[0, 0][None, :] * projected
    mlp_in = modulate_rows(hidden, mlp_shift[0, 0], mlp_scale[0, 0])
    n_y = lax.axis_size("ry")
    pair = [(0, 1), (1, 0)]
    up_other = lax.ppermute(w_up, "rc", pair)
    down_other = lax.ppermute(w_down, "rc", pair)
    line_in = lax.all_gather(mlp_in, "ry", axis=0, tiled=True)
    inner_own = jax.nn.gelu(
        jnp.dot(line_in, w_up, preferred_element_type=jnp.float32), approximate=True
    ).astype(jnp.bfloat16)
    inner_other = jax.nn.gelu(
        jnp.dot(line_in, up_other, preferred_element_type=jnp.float32), approximate=True
    ).astype(jnp.bfloat16)
    mlp_parts = (
        (
            jnp.dot(inner_own, w_down, preferred_element_type=jnp.float32)
            + jnp.dot(inner_other, down_other, preferred_element_type=jnp.float32)
        )
        .astype(jnp.bfloat16)
        .reshape(n_y, img_dev, w_down.shape[1])
    )
    mlp_out = jnp.sum(
        lax.all_to_all(mlp_parts, "ry", 0, 0, tiled=True).astype(jnp.float32), axis=0
    )
    hidden_two = hidden + mlp_gate[0, 0][None, :] * mlp_out
    modulated = modulate_rows(hidden_two, shift[0, 0], scale[0, 0])
    velocity = jnp.dot(modulated, w_out, preferred_element_type=jnp.float32)
    n_cfg = lax.axis_size("cfg")
    half_width = velocity.shape[1] // n_cfg
    side_index = lax.axis_index("cfg")
    n_seq = lax.axis_size(("sz", "sx"))
    seq_index = lax.axis_index(("sz", "sx"))
    everything = lax.all_to_all(
        jnp.broadcast_to(velocity[None], (n_cfg * n_seq,) + velocity.shape),
        ("cfg", "sz", "sx"),
        0,
        0,
        tiled=True,
    ).reshape(n_cfg, n_seq, img_dev, velocity.shape[1])
    cond_part = everything[0]
    uncond = everything[1]
    guided_all = uncond + guidance_weight * (cond_part - uncond)
    guided_total = jnp.sum(guided_all * guided_all)
    peak_value = jnp.max(jnp.abs(guided_all))
    entries = img_dev * n_seq * velocity.shape[1]
    guided_norm = jnp.sqrt(guided_total / entries + 1e-06)
    guided_rows = lax.dynamic_index_in_dim(guided_all, seq_index, 0, keepdims=False)
    guided = lax.dynamic_slice_in_dim(guided_rows, side_index * half_width, half_width, 1)
    latent_next = latent + step_size[0] * guided[None, :, :]
    return (latent_next, jnp.reshape(guided_norm, (1,)), jnp.reshape(peak_value, (1,)))


def solution(mesh):
    n_seq = mesh.shape["seq"]
    n_req = mesh.shape["req"]
    n_x = SEQ_MINOR if n_seq % SEQ_MINOR == 0 else 1
    n_core = CORES if n_req % CORES == 0 else 1
    split_mesh = Mesh(
        mesh.devices.reshape(mesh.shape["cfg"], n_req // n_core, n_core, n_seq // n_x, n_x),
        ("cfg", "ry", "rc", "sz", "sx"),
    )
    req = ("ry", "rc")
    seq = ("sz", "sx")
    in_specs = (
        P("cfg", req, seq, None),
        P(None, "cfg", req, seq, None),
        P("cfg", req, seq, None),
        P("cfg", req),
        P("cfg", req, None),
        P("cfg", req, None),
        P("cfg", req, None),
        P("cfg", req, None),
        P("cfg", req, None),
        P("cfg", req, None),
        P(None, req),
        P(None, req),
        P(req, None),
        P(),
        P(req, seq, "cfg"),
        P(req),
    )
    out_specs = (P(req, seq, "cfg"), P(req), P(req))
    return jax.shard_map(
        per_device, mesh=split_mesh, in_specs=in_specs, out_specs=out_specs, check_vma=False
    )
```

```python
import jax
import jax.numpy as jnp
from jax import lax
from jax.sharding import Mesh, PartitionSpec as P

HEADS = 12
HD = 64
SEQ_MINOR = 4
CORES = 2


guidance_weight = 4.0


def swapped(block, axis, apart):
    count = lax.axis_size(axis)
    route = []
    for low in range(count):
        high = low | 1 << apart
        if high != low and high < count:
            route += [(low, high), (high, low)]
    return lax.ppermute(block, axis, route)


def modulate_rows(hidden, shift_row, scale_row):
    row_mean = jnp.mean(hidden, axis=1, keepdims=True)
    centered = hidden - row_mean
    row_var = jnp.mean(centered * centered, axis=1, keepdims=True)
    return (
        centered * lax.rsqrt(row_var + 1e-06) * (1.0 + scale_row[None, :]) + shift_row[None, :]
    ).astype(jnp.bfloat16)


def per_device(
    query,
    key_value,
    residual_in,
    text_len,
    attn_gate,
    mlp_shift,
    mlp_scale,
    mlp_gate,
    shift,
    scale,
    w_proj,
    w_up,
    w_down,
    w_out,
    latent,
    step_size,
):
    img_dev = query.shape[2]
    rows_dev = key_value.shape[3]
    txt_dev = rows_dev - img_dev
    length = text_len[0, 0]
    factor = HD ** (-0.5)
    n_x = lax.axis_size("sx")
    x_index = lax.axis_index("sx")
    query_rows = lax.all_to_all(
        jnp.broadcast_to(query[0, 0][None], (n_x,) + query.shape[2:]), "sx", 0, 0, tiled=True
    ).reshape(n_x * img_dev, query.shape[3])
    piece = lax.all_gather(key_value[:, 0, 0], "sz", axis=1, tiled=True)
    q_rows = query_rows.shape[0]
    piece_rows = piece.shape[1]
    positions = jnp.arange(piece_rows, dtype=jnp.int32)
    within = positions % rows_dev
    source = (positions // rows_dev) * n_x + x_index
    text_slot = source * txt_dev + within - img_dev
    usable = ((within < img_dev) | (text_slot < length))[None, None, :]
    queries = query_rows.reshape(q_rows, HEADS, HD)
    keys_here = piece[0].reshape(piece_rows, HEADS, HD)
    vals_here = piece[1].reshape(piece_rows, HEADS, HD)
    logits = (
        jnp.einsum("qhd,khd->qhk", queries, keys_here, preferred_element_type=jnp.float32) * factor
    )
    part_max = jnp.max(jnp.where(usable, logits, -1e30), axis=2)
    weights = jnp.where(usable, jnp.exp(logits - part_max[:, :, None]), 0.0)
    part_sum = jnp.sum(weights, axis=2)
    weighted = jnp.einsum(
        "qhk,khd->qhd", weights.astype(jnp.bfloat16), vals_here, preferred_element_type=jnp.float32
    )
    width = HEADS * HD
    packed = jnp.concatenate(
        [weighted.reshape(q_rows, width), part_max, part_sum], axis=1
    ).reshape(n_x, img_dev, width + 2 * HEADS)
    got = lax.all_to_all(packed, "sx", 0, 0, tiled=True)
    got_out = got[:, :, :width].reshape(n_x, img_dev, HEADS, HD)
    got_max = got[:, :, width : width + HEADS]
    got_sum = got[:, :, width + HEADS :]
    row_max = jnp.max(got_max, axis=0)
    rescale = jnp.exp(got_max - row_max[None])
    numerator = jnp.sum(rescale[:, :, :, None] * got_out, axis=0)
    denominator = jnp.sum(rescale * got_sum, axis=0)
    attended = (numerator / denominator[:, :, None]).reshape(img_dev, width).astype(jnp.bfloat16)
    projected = jnp.dot(
        attended,
        lax.all_gather(w_proj, ("ry", "rc"), axis=1, tiled=True),
        preferred_element_type=jnp.float32,
    )
    hidden = residual_in[0, 0].astype(jnp.float32) + attn_gate[0, 0][None, :] * projected
    mlp_in = modulate_rows(hidden, mlp_shift[0, 0], mlp_scale[0, 0])
    n_y = lax.axis_size("ry")
    pair = [(0, 1), (1, 0)]
    up_other = lax.ppermute(w_up, "rc", pair)
    down_other = lax.ppermute(w_down, "rc", pair)
    y_index = lax.axis_index("ry")
    shifts = range(1, n_y)
    line_blocks = jnp.stack(
        [mlp_in]
        + [lax.ppermute(mlp_in, "ry", [(i, (i + k) % n_y) for i in range(n_y)]) for k in shifts]
    )
    line_in = line_blocks.reshape(n_y * img_dev, mlp_in.shape[1])
    inner_own = jax.nn.gelu(
        jnp.dot(line_in, w_up, preferred_element_type=jnp.float32), approximate=True
    ).astype(jnp.bfloat16)
    inner_other = jax.nn.gelu(
        jnp.dot(line_in, up_other, preferred_element_type=jnp.float32), approximate=True
    ).astype(jnp.bfloat16)
    mlp_parts = (
        (
            jnp.dot(inner_own, w_down, preferred_element_type=jnp.float32)
            + jnp.dot(inner_other, down_other, preferred_element_type=jnp.float32)
        )
        .astype(jnp.bfloat16)
        .reshape(n_y, img_dev, w_down.shape[1])
    )
    mlp_total = mlp_parts[0].astype(jnp.float32)
    for k in shifts:
        mlp_total = mlp_total + lax.ppermute(
            mlp_parts[k], "ry", [(i, (i - k) % n_y) for i in range(n_y)]
        ).astype(jnp.float32)
    mlp_out = mlp_total
    hidden_two = hidden + mlp_gate[0, 0][None, :] * mlp_out
    modulated = modulate_rows(hidden_two, shift[0, 0], scale[0, 0])
    velocity = jnp.dot(modulated, w_out, preferred_element_type=jnp.float32)
    half_width = velocity.shape[1] // lax.axis_size("cfg")
    side_index = lax.axis_index("cfg")
    received = swapped(velocity, "cfg", 0)
    is_cond = side_index == 0
    cond_part = jnp.where(is_cond, velocity, received)
    uncond = jnp.where(is_cond, received, velocity)
    guided_full = uncond + guidance_weight * (cond_part - uncond)
    partials = jnp.stack([jnp.sum(guided_full * guided_full), jnp.max(jnp.abs(guided_full))])
    n_seq = lax.axis_size(("sz", "sx"))
    gathered = lax.all_to_all(
        jnp.broadcast_to(partials[None], (n_seq, 2)), ("sz", "sx"), 0, 0, tiled=True
    )
    guided_total = jnp.sum(gathered[:, 0])
    peak_value = jnp.max(gathered[:, 1])
    entries = img_dev * n_seq * velocity.shape[1]
    guided_norm = jnp.sqrt(guided_total / entries + 1e-06)
    guided = lax.dynamic_slice_in_dim(guided_full, side_index * half_width, half_width, 1)
    latent_next = latent + step_size[0] * guided[None, :, :]
    return (latent_next, jnp.reshape(guided_norm, (1,)), jnp.reshape(peak_value, (1,)))


def solution(mesh):
    n_seq = mesh.shape["seq"]
    n_req = mesh.shape["req"]
    n_x = SEQ_MINOR if n_seq % SEQ_MINOR == 0 else 1
    n_core = CORES if n_req % CORES == 0 else 1
    split_mesh = Mesh(
        mesh.devices.reshape(mesh.shape["cfg"], n_req // n_core, n_core, n_seq // n_x, n_x),
        ("cfg", "ry", "rc", "sz", "sx"),
    )
    req = ("ry", "rc")
    seq = ("sz", "sx")
    in_specs = (
        P("cfg", req, seq, None),
        P(None, "cfg", req, seq, None),
        P("cfg", req, seq, None),
        P("cfg", req),
        P("cfg", req, None),
        P("cfg", req, None),
        P("cfg", req, None),
        P("cfg", req, None),
        P("cfg", req, None),
        P("cfg", req, None),
        P(None, req),
        P(None, req),
        P(req, None),
        P(),
        P(req, seq, "cfg"),
        P(req),
    )
    out_specs = (P(req, seq, "cfg"), P(req), P(req))
    return jax.shard_map(
        per_device, mesh=split_mesh, in_specs=in_specs, out_specs=out_specs, check_vma=False
    )
```

```python
import jax
import jax.numpy as jnp
from jax import lax
from jax.experimental import pallas as pl
from jax.experimental.pallas import tpu as pltpu
from jax.sharding import Mesh, PartitionSpec as P

HEADS = 12
HD = 64
SEQ_MINOR = 4
CORES = 2


guidance_weight = 4.0


def swapped(block, axis, apart):
    count = lax.axis_size(axis)
    route = []
    for low in range(count):
        high = low | 1 << apart
        if high != low and high < count:
            route += [(low, high), (high, low)]
    return lax.ppermute(block, axis, route)


def attention_partials_kernel(q_ref, kv_ref, mask_ref, out_ref):
    rows = q_ref.shape[0]
    lanes = 2 * HD
    lane = lax.broadcasted_iota(jnp.int32, (1, lanes), 1)
    low = lane < HD
    usable = mask_ref[...] > 0
    factor = HD ** (-0.5)
    maxes = []
    sums = []
    for pair in range(HEADS // 2):
        cols = slice(pair * lanes, (pair + 1) * lanes)
        q2 = q_ref[:, cols]
        k2 = kv_ref[0, :, cols]
        v2 = kv_ref[1, :, cols]
        outs = []
        for half in (low, jnp.logical_not(low)):
            q_half = jnp.where(half, q2, jnp.zeros_like(q2))
            logits = lax.dot_general(
                q_half, k2, (((1,), (1,)), ((), ())), preferred_element_type=jnp.float32
            ) * factor
            part_max = jnp.max(jnp.where(usable, logits, -1e30), axis=1, keepdims=True)
            weights = jnp.where(usable, jnp.exp(logits - part_max), 0.0)
            sums.append(jnp.sum(weights, axis=1, keepdims=True))
            maxes.append(part_max)
            outs.append(
                jnp.dot(weights.astype(jnp.bfloat16), v2, preferred_element_type=jnp.float32)
            )
        out_ref[:, cols] = jnp.where(low, outs[0], outs[1])
    width = HEADS * HD
    out_ref[:, width : width + HEADS] = jnp.concatenate(maxes, axis=1)
    out_ref[:, width + HEADS : width + 2 * HEADS] = jnp.concatenate(sums, axis=1)

def attention_partials(q, kv, mask):
    rows = q.shape[0]
    width = HEADS * HD
    return pl.pallas_call(
        attention_partials_kernel,
        out_shape=jax.ShapeDtypeStruct((rows, width + 2 * HEADS), jnp.float32),
        in_specs=[pl.BlockSpec(memory_space=pltpu.VMEM)] * 3,
        out_specs=pl.BlockSpec(memory_space=pltpu.VMEM),
        cost_estimate=pl.CostEstimate(
            flops=8 * rows * kv.shape[1] * width,
            transcendentals=2 * rows * kv.shape[1] * HEADS,
            bytes_accessed=q.size * 2 + kv.size * 2 + rows * (width + 2 * HEADS) * 4,
        ),
    )(q, kv, mask)


def modulate_rows(hidden, shift_row, scale_row):
    row_mean = jnp.mean(hidden, axis=1, keepdims=True)
    centered = hidden - row_mean
    row_var = jnp.mean(centered * centered, axis=1, keepdims=True)
    return (
        centered * lax.rsqrt(row_var + 1e-06) * (1.0 + scale_row[None, :]) + shift_row[None, :]
    ).astype(jnp.bfloat16)


def per_device(
    query,
    key_value,
    residual_in,
    text_len,
    attn_gate,
    mlp_shift,
    mlp_scale,
    mlp_gate,
    shift,
    scale,
    w_proj,
    w_up,
    w_down,
    w_out,
    latent,
    step_size,
):
    img_dev = query.shape[2]
    rows_dev = key_value.shape[3]
    txt_dev = rows_dev - img_dev
    length = text_len[0, 0]
    factor = HD ** (-0.5)
    n_x = lax.axis_size("sx")
    x_index = lax.axis_index("sx")
    query_rows = lax.all_to_all(
        jnp.broadcast_to(query[0, 0][None], (n_x,) + query.shape[2:]), "sx", 0, 0, tiled=True
    ).reshape(n_x * img_dev, query.shape[3])
    piece = lax.all_gather(key_value[:, 0, 0], "sz", axis=1, tiled=True)
    q_rows = query_rows.shape[0]
    piece_rows = piece.shape[1]
    positions = jnp.arange(piece_rows, dtype=jnp.int32)
    within = positions % rows_dev
    source = (positions // rows_dev) * n_x + x_index
    text_slot = source * txt_dev + within - img_dev
    usable = ((within < img_dev) | (text_slot < length)).astype(jnp.float32)[None, :]
    width = HEADS * HD
    packed = attention_partials(
        query_rows, piece.reshape(2, piece_rows, width), usable
    ).reshape(n_x, img_dev, width + 2 * HEADS)
    got = lax.all_to_all(packed, "sx", 0, 0, tiled=True)
    got_out = got[:, :, :width].reshape(n_x, img_dev, HEADS, HD)
    got_max = got[:, :, width : width + HEADS]
    got_sum = got[:, :, width + HEADS :]
    row_max = jnp.max(got_max, axis=0)
    rescale = jnp.exp(got_max - row_max[None])
    numerator = jnp.sum(rescale[:, :, :, None] * got_out, axis=0)
    denominator = jnp.sum(rescale * got_sum, axis=0)
    attended = (numerator / denominator[:, :, None]).reshape(img_dev, width).astype(jnp.bfloat16)
    projected = jnp.dot(
        attended,
        lax.all_gather(w_proj, ("ry", "rc"), axis=1, tiled=True),
        preferred_element_type=jnp.float32,
    )
    hidden = residual_in[0, 0].astype(jnp.float32) + attn_gate[0, 0][None, :] * projected
    mlp_in = modulate_rows(hidden, mlp_shift[0, 0], mlp_scale[0, 0])
    n_y = lax.axis_size("ry")
    pair = [(0, 1), (1, 0)]
    up_other = lax.ppermute(w_up, "rc", pair)
    down_other = lax.ppermute(w_down, "rc", pair)
    line_in = lax.all_gather(mlp_in, "ry", axis=0, tiled=True)
    inner_own = jax.nn.gelu(
        jnp.dot(line_in, w_up, preferred_element_type=jnp.float32), approximate=True
    ).astype(jnp.bfloat16)
    inner_other = jax.nn.gelu(
        jnp.dot(line_in, up_other, preferred_element_type=jnp.float32), approximate=True
    ).astype(jnp.bfloat16)
    mlp_parts = (
        (
            jnp.dot(inner_own, w_down, preferred_element_type=jnp.float32)
            + jnp.dot(inner_other, down_other, preferred_element_type=jnp.float32)
        )
        .astype(jnp.bfloat16)
        .reshape(n_y, img_dev, w_down.shape[1])
    )
    mlp_out = jnp.sum(
        lax.all_to_all(mlp_parts, "ry", 0, 0, tiled=True).astype(jnp.float32), axis=0
    )
    hidden_two = hidden + mlp_gate[0, 0][None, :] * mlp_out
    modulated = modulate_rows(hidden_two, shift[0, 0], scale[0, 0])
    velocity = jnp.dot(modulated, w_out, preferred_element_type=jnp.float32)
    half_width = velocity.shape[1] // lax.axis_size("cfg")
    side_index = lax.axis_index("cfg")
    received = swapped(velocity, "cfg", 0)
    is_cond = side_index == 0
    cond_part = jnp.where(is_cond, velocity, received)
    uncond = jnp.where(is_cond, received, velocity)
    guided_full = uncond + guidance_weight * (cond_part - uncond)
    partials = jnp.stack([jnp.sum(guided_full * guided_full), jnp.max(jnp.abs(guided_full))])
    n_seq = lax.axis_size(("sz", "sx"))
    gathered = lax.all_to_all(
        jnp.broadcast_to(partials[None], (n_seq, 2)), ("sz", "sx"), 0, 0, tiled=True
    )
    guided_total = jnp.sum(gathered[:, 0])
    peak_value = jnp.max(gathered[:, 1])
    entries = img_dev * n_seq * velocity.shape[1]
    guided_norm = jnp.sqrt(guided_total / entries + 1e-06)
    guided = lax.dynamic_slice_in_dim(guided_full, side_index * half_width, half_width, 1)
    latent_next = latent + step_size[0] * guided[None, :, :]
    return (latent_next, jnp.reshape(guided_norm, (1,)), jnp.reshape(peak_value, (1,)))


def solution(mesh):
    n_seq = mesh.shape["seq"]
    n_req = mesh.shape["req"]
    n_x = SEQ_MINOR if n_seq % SEQ_MINOR == 0 else 1
    n_core = CORES if n_req % CORES == 0 else 1
    split_mesh = Mesh(
        mesh.devices.reshape(mesh.shape["cfg"], n_req // n_core, n_core, n_seq // n_x, n_x),
        ("cfg", "ry", "rc", "sz", "sx"),
    )
    req = ("ry", "rc")
    seq = ("sz", "sx")
    in_specs = (
        P("cfg", req, seq, None),
        P(None, "cfg", req, seq, None),
        P("cfg", req, seq, None),
        P("cfg", req),
        P("cfg", req, None),
        P("cfg", req, None),
        P("cfg", req, None),
        P("cfg", req, None),
        P("cfg", req, None),
        P("cfg", req, None),
        P(None, req),
        P(None, req),
        P(req, None),
        P(),
        P(req, seq, "cfg"),
        P(req),
    )
    out_specs = (P(req, seq, "cfg"), P(req), P(req))
    return jax.shard_map(
        per_device, mesh=split_mesh, in_specs=in_specs, out_specs=out_specs, check_vma=False
    )
```

```python
import jax
import jax.numpy as jnp
from jax import lax
from jax.experimental import pallas as pl
from jax.experimental.pallas import tpu as pltpu
from jax.sharding import Mesh, PartitionSpec as P

HEADS = 12
HD = 64
SEQ_MINOR = 4
CORES = 2


guidance_weight = 4.0


def swapped(block, axis, apart):
    count = lax.axis_size(axis)
    route = []
    for low in range(count):
        high = low | 1 << apart
        if high != low and high < count:
            route += [(low, high), (high, low)]
    return lax.ppermute(block, axis, route)


def attention_partials_kernel(q_ref, kv_ref, mask_ref, out_ref):
    rows = q_ref.shape[0]
    lanes = 2 * HD
    lane = lax.broadcasted_iota(jnp.int32, (1, lanes), 1)
    low = lane < HD
    usable = mask_ref[...] > 0
    factor = HD ** (-0.5)
    maxes = []
    sums = []
    for pair in range(HEADS // 2):
        cols = slice(pair * lanes, (pair + 1) * lanes)
        q2 = q_ref[:, cols]
        k2 = kv_ref[0, :, cols]
        v2 = kv_ref[1, :, cols]
        outs = []
        for half in (low, jnp.logical_not(low)):
            q_half = jnp.where(half, q2, jnp.zeros_like(q2))
            logits = lax.dot_general(
                q_half, k2, (((1,), (1,)), ((), ())), preferred_element_type=jnp.float32
            ) * factor
            part_max = jnp.max(jnp.where(usable, logits, -1e30), axis=1, keepdims=True)
            weights = jnp.where(usable, jnp.exp(logits - part_max), 0.0)
            sums.append(jnp.sum(weights, axis=1, keepdims=True))
            maxes.append(part_max)
            outs.append(
                jnp.dot(weights.astype(jnp.bfloat16), v2, preferred_element_type=jnp.float32)
            )
        out_ref[:, cols] = jnp.where(low, outs[0], outs[1])
    width = HEADS * HD
    out_ref[:, width : width + HEADS] = jnp.concatenate(maxes, axis=1)
    out_ref[:, width + HEADS : width + 2 * HEADS] = jnp.concatenate(sums, axis=1)

def attention_partials(q, kv, mask):
    rows = q.shape[0]
    width = HEADS * HD
    return pl.pallas_call(
        attention_partials_kernel,
        out_shape=jax.ShapeDtypeStruct((rows, width + 2 * HEADS), jnp.float32),
        in_specs=[pl.BlockSpec(memory_space=pltpu.VMEM)] * 3,
        out_specs=pl.BlockSpec(memory_space=pltpu.VMEM),
        cost_estimate=pl.CostEstimate(
            flops=8 * rows * kv.shape[1] * width,
            transcendentals=2 * rows * kv.shape[1] * HEADS,
            bytes_accessed=q.size * 2 + kv.size * 2 + rows * (width + 2 * HEADS) * 4,
        ),
    )(q, kv, mask)


def modulate_rows(hidden, shift_row, scale_row):
    row_mean = jnp.mean(hidden, axis=1, keepdims=True)
    centered = hidden - row_mean
    row_var = jnp.mean(centered * centered, axis=1, keepdims=True)
    return (
        centered * lax.rsqrt(row_var + 1e-06) * (1.0 + scale_row[None, :]) + shift_row[None, :]
    ).astype(jnp.bfloat16)


def per_device(
    query,
    key_value,
    residual_in,
    text_len,
    attn_gate,
    mlp_shift,
    mlp_scale,
    mlp_gate,
    shift,
    scale,
    w_proj,
    w_up,
    w_down,
    w_out,
    latent,
    step_size,
):
    img_dev = query.shape[2]
    rows_dev = key_value.shape[3]
    txt_dev = rows_dev - img_dev
    length = text_len[0, 0]
    factor = HD ** (-0.5)
    n_x = lax.axis_size("sx")
    x_index = lax.axis_index("sx")
    query_rows = lax.all_to_all(
        jnp.broadcast_to(query[0, 0][None], (n_x,) + query.shape[2:]), "sx", 0, 0, tiled=True
    ).reshape(n_x * img_dev, query.shape[3])
    piece = lax.all_gather(key_value[:, 0, 0], "sz", axis=1, tiled=True)
    q_rows = query_rows.shape[0]
    piece_rows = piece.shape[1]
    positions = jnp.arange(piece_rows, dtype=jnp.int32)
    within = positions % rows_dev
    source = (positions // rows_dev) * n_x + x_index
    text_slot = source * txt_dev + within - img_dev
    usable = ((within < img_dev) | (text_slot < length)).astype(jnp.float32)[None, :]
    width = HEADS * HD
    packed = attention_partials(
        query_rows, piece.reshape(2, piece_rows, width), usable
    ).reshape(n_x, img_dev, width + 2 * HEADS)
    got = lax.all_to_all(packed, "sx", 0, 0, tiled=True)
    got_out = got[:, :, :width].reshape(n_x, img_dev, HEADS, HD)
    got_max = got[:, :, width : width + HEADS]
    got_sum = got[:, :, width + HEADS :]
    row_max = jnp.max(got_max, axis=0)
    rescale = jnp.exp(got_max - row_max[None])
    numerator = jnp.sum(rescale[:, :, :, None] * got_out, axis=0)
    denominator = jnp.sum(rescale * got_sum, axis=0)
    attended = (numerator / denominator[:, :, None]).reshape(img_dev, width).astype(jnp.bfloat16)
    projected = jnp.dot(
        attended,
        lax.all_gather(w_proj, ("ry", "rc"), axis=1, tiled=True),
        preferred_element_type=jnp.float32,
    )
    hidden = residual_in[0, 0].astype(jnp.float32) + attn_gate[0, 0][None, :] * projected
    mlp_in = modulate_rows(hidden, mlp_shift[0, 0], mlp_scale[0, 0])
    n_y = lax.axis_size("ry")
    pair = [(0, 1), (1, 0)]
    up_other = lax.ppermute(w_up, "rc", pair)
    down_other = lax.ppermute(w_down, "rc", pair)
    line_in = lax.all_gather(mlp_in, "ry", axis=0, tiled=True)
    inner_own = jax.nn.gelu(
        jnp.dot(line_in, w_up, preferred_element_type=jnp.float32), approximate=True
    ).astype(jnp.bfloat16)
    inner_other = jax.nn.gelu(
        jnp.dot(line_in, up_other, preferred_element_type=jnp.float32), approximate=True
    ).astype(jnp.bfloat16)
    mlp_parts = (
        (
            jnp.dot(inner_own, w_down, preferred_element_type=jnp.float32)
            + jnp.dot(inner_other, down_other, preferred_element_type=jnp.float32)
        )
        .astype(jnp.bfloat16)
        .reshape(n_y, img_dev, w_down.shape[1])
    )
    mlp_out = jnp.sum(
        lax.all_to_all(mlp_parts, "ry", 0, 0, tiled=True).astype(jnp.float32), axis=0
    )
    hidden_two = hidden + mlp_gate[0, 0][None, :] * mlp_out
    modulated = modulate_rows(hidden_two, shift[0, 0], scale[0, 0])
    velocity = jnp.dot(modulated, w_out, preferred_element_type=jnp.float32)
    half_width = velocity.shape[1] // lax.axis_size("cfg")
    side_index = lax.axis_index("cfg")
    n_cfg = lax.axis_size("cfg")
    halves = lax.all_to_all(
        jnp.broadcast_to(velocity[None], (n_cfg,) + velocity.shape), "cfg", 0, 0, tiled=True
    )
    cond_part = halves[0]
    uncond = halves[1]
    guided_full = uncond + guidance_weight * (cond_part - uncond)
    partials = jnp.stack([jnp.sum(guided_full * guided_full), jnp.max(jnp.abs(guided_full))])
    n_seq = lax.axis_size(("sz", "sx"))
    gathered = lax.all_to_all(
        jnp.broadcast_to(partials[None], (n_seq, 2)), ("sz", "sx"), 0, 0, tiled=True
    )
    guided_total = jnp.sum(gathered[:, 0])
    peak_value = jnp.max(gathered[:, 1])
    entries = img_dev * n_seq * velocity.shape[1]
    guided_norm = jnp.sqrt(guided_total / entries + 1e-06)
    guided = lax.dynamic_slice_in_dim(guided_full, side_index * half_width, half_width, 1)
    latent_next = latent + step_size[0] * guided[None, :, :]
    return (latent_next, jnp.reshape(guided_norm, (1,)), jnp.reshape(peak_value, (1,)))


def solution(mesh):
    n_seq = mesh.shape["seq"]
    n_req = mesh.shape["req"]
    n_x = SEQ_MINOR if n_seq % SEQ_MINOR == 0 else 1
    n_core = CORES if n_req % CORES == 0 else 1
    split_mesh = Mesh(
        mesh.devices.reshape(mesh.shape["cfg"], n_req // n_core, n_core, n_seq // n_x, n_x),
        ("cfg", "ry", "rc", "sz", "sx"),
    )
    req = ("ry", "rc")
    seq = ("sz", "sx")
    in_specs = (
        P("cfg", req, seq, None),
        P(None, "cfg", req, seq, None),
        P("cfg", req, seq, None),
        P("cfg", req),
        P("cfg", req, None),
        P("cfg", req, None),
        P("cfg", req, None),
        P("cfg", req, None),
        P("cfg", req, None),
        P("cfg", req, None),
        P(None, req),
        P(None, req),
        P(req, None),
        P(),
        P(req, seq, "cfg"),
        P(req),
    )
    out_specs = (P(req, seq, "cfg"), P(req), P(req))
    return jax.shard_map(
        per_device, mesh=split_mesh, in_specs=in_specs, out_specs=out_specs, check_vma=False
    )
```

```python
import functools

import jax
import jax.numpy as jnp
from jax import lax
from jax.experimental import pallas as pl
from jax.experimental.pallas import tpu as pltpu
from jax.sharding import Mesh, PartitionSpec as P

HEADS = 12
HD = 64
SEQ_MINOR = 4
CORES = 2


guidance_weight = 4.0


def swapped(block, axis, apart):
    count = lax.axis_size(axis)
    route = []
    for low in range(count):
        high = low | 1 << apart
        if high != low and high < count:
            route += [(low, high), (high, low)]
    return lax.ppermute(block, axis, route)


def attention_partials_kernel(rows_dev, img_dev, n_x, q_ref, kv_ref, info_ref, out_ref):
    rows = q_ref.shape[0]
    lanes = 2 * HD
    lane = lax.broadcasted_iota(jnp.int32, (1, lanes), 1)
    low = lane < HD
    keys = kv_ref.shape[1]
    position = lax.broadcasted_iota(jnp.int32, (1, keys), 1)
    within = position % rows_dev
    source = (position // rows_dev) * n_x + info_ref[0:1, 1:2]
    text_slot = source * (rows_dev - img_dev) + within - img_dev
    usable = (within < img_dev) | (text_slot < info_ref[0:1, 0:1])
    factor = HD ** (-0.5)
    maxes = []
    sums = []
    for pair in range(HEADS // 2):
        cols = slice(pair * lanes, (pair + 1) * lanes)
        q2 = q_ref[:, cols]
        k2 = kv_ref[0, :, cols]
        v2 = kv_ref[1, :, cols]
        outs = []
        for half in (low, jnp.logical_not(low)):
            q_half = jnp.where(half, q2, jnp.zeros_like(q2))
            logits = lax.dot_general(
                q_half, k2, (((1,), (1,)), ((), ())), preferred_element_type=jnp.float32
            ) * factor
            part_max = jnp.max(jnp.where(usable, logits, -1e30), axis=1, keepdims=True)
            weights = jnp.where(usable, jnp.exp(logits - part_max), 0.0)
            sums.append(jnp.sum(weights, axis=1, keepdims=True))
            maxes.append(part_max)
            outs.append(
                jnp.dot(weights.astype(jnp.bfloat16), v2, preferred_element_type=jnp.float32)
            )
        out_ref[:, cols] = jnp.where(low, outs[0], outs[1])
    width = HEADS * HD
    out_ref[:, width : width + HEADS] = jnp.concatenate(maxes, axis=1)
    out_ref[:, width + HEADS : width + 2 * HEADS] = jnp.concatenate(sums, axis=1)

def attention_partials(q, kv, info, rows_dev, img_dev, n_x):
    rows = q.shape[0]
    width = HEADS * HD
    return pl.pallas_call(
        functools.partial(attention_partials_kernel, rows_dev, img_dev, n_x),
        out_shape=jax.ShapeDtypeStruct((rows, width + 2 * HEADS), jnp.float32),
        in_specs=[pl.BlockSpec(memory_space=pltpu.VMEM)] * 3,
        out_specs=pl.BlockSpec(memory_space=pltpu.VMEM),
        cost_estimate=pl.CostEstimate(
            flops=8 * rows * kv.shape[1] * width,
            transcendentals=2 * rows * kv.shape[1] * HEADS,
            bytes_accessed=q.size * 2 + kv.size * 2 + rows * (width + 2 * HEADS) * 4,
        ),
    )(q, kv, info)


def modulate_rows(hidden, shift_row, scale_row):
    row_mean = jnp.mean(hidden, axis=1, keepdims=True)
    centered = hidden - row_mean
    row_var = jnp.mean(centered * centered, axis=1, keepdims=True)
    return (
        centered * lax.rsqrt(row_var + 1e-06) * (1.0 + scale_row[None, :]) + shift_row[None, :]
    ).astype(jnp.bfloat16)


def per_device(
    query,
    key_value,
    residual_in,
    text_len,
    attn_gate,
    mlp_shift,
    mlp_scale,
    mlp_gate,
    shift,
    scale,
    w_proj,
    w_up,
    w_down,
    w_out,
    latent,
    step_size,
):
    img_dev = query.shape[2]
    rows_dev = key_value.shape[3]
    txt_dev = rows_dev - img_dev
    length = text_len[0, 0]
    factor = HD ** (-0.5)
    n_x = lax.axis_size("sx")
    x_index = lax.axis_index("sx")
    query_rows = lax.all_to_all(
        jnp.broadcast_to(query[0, 0][None], (n_x,) + query.shape[2:]), "sx", 0, 0, tiled=True
    ).reshape(n_x * img_dev, query.shape[3])
    piece = lax.all_gather(key_value[:, 0, 0], "sz", axis=1, tiled=True)
    q_rows = query_rows.shape[0]
    piece_rows = piece.shape[1]
    width = HEADS * HD
    info = jnp.stack([length, x_index.astype(jnp.int32)]).reshape(1, 2)
    packed = attention_partials(
        query_rows, piece.reshape(2, piece_rows, width), info, rows_dev, img_dev, n_x
    ).reshape(n_x, img_dev, width + 2 * HEADS)
    got = lax.all_to_all(packed, "sx", 0, 0, tiled=True)
    got_out = got[:, :, :width].reshape(n_x, img_dev, HEADS, HD)
    got_max = got[:, :, width : width + HEADS]
    got_sum = got[:, :, width + HEADS :]
    row_max = jnp.max(got_max, axis=0)
    rescale = jnp.exp(got_max - row_max[None])
    numerator = jnp.sum(rescale[:, :, :, None] * got_out, axis=0)
    denominator = jnp.sum(rescale * got_sum, axis=0)
    attended = (numerator / denominator[:, :, None]).reshape(img_dev, width).astype(jnp.bfloat16)
    projected = jnp.dot(
        attended,
        lax.all_gather(w_proj, ("ry", "rc"), axis=1, tiled=True),
        preferred_element_type=jnp.float32,
    )
    hidden = residual_in[0, 0].astype(jnp.float32) + attn_gate[0, 0][None, :] * projected
    mlp_in = modulate_rows(hidden, mlp_shift[0, 0], mlp_scale[0, 0])
    n_y = lax.axis_size("ry")
    pair = [(0, 1), (1, 0)]
    up_other = lax.ppermute(w_up, "rc", pair)
    down_other = lax.ppermute(w_down, "rc", pair)
    line_in = lax.all_gather(mlp_in, "ry", axis=0, tiled=True)
    inner_own = jax.nn.gelu(
        jnp.dot(line_in, w_up, preferred_element_type=jnp.float32), approximate=True
    ).astype(jnp.bfloat16)
    inner_other = jax.nn.gelu(
        jnp.dot(line_in, up_other, preferred_element_type=jnp.float32), approximate=True
    ).astype(jnp.bfloat16)
    mlp_parts = (
        (
            jnp.dot(inner_own, w_down, preferred_element_type=jnp.float32)
            + jnp.dot(inner_other, down_other, preferred_element_type=jnp.float32)
        )
        .astype(jnp.bfloat16)
        .reshape(n_y, img_dev, w_down.shape[1])
    )
    mlp_out = jnp.sum(
        lax.all_to_all(mlp_parts, "ry", 0, 0, tiled=True).astype(jnp.float32), axis=0
    )
    hidden_two = hidden + mlp_gate[0, 0][None, :] * mlp_out
    modulated = modulate_rows(hidden_two, shift[0, 0], scale[0, 0])
    velocity = jnp.dot(modulated, w_out, preferred_element_type=jnp.float32)
    half_width = velocity.shape[1] // lax.axis_size("cfg")
    side_index = lax.axis_index("cfg")
    received = swapped(velocity, "cfg", 0)
    is_cond = side_index == 0
    cond_part = jnp.where(is_cond, velocity, received)
    uncond = jnp.where(is_cond, received, velocity)
    guided_full = uncond + guidance_weight * (cond_part - uncond)
    square_sum, largest = lax.reduce(
        (guided_full * guided_full, jnp.abs(guided_full)),
        (jnp.float32(0), jnp.float32(0)),
        lambda a, b: (a[0] + b[0], jnp.maximum(a[1], b[1])),
        (0, 1),
    )
    partials = jnp.stack([square_sum, largest])
    n_seq = lax.axis_size(("sz", "sx"))
    gathered = lax.all_to_all(
        jnp.broadcast_to(partials[None], (n_seq, 2)), ("sz", "sx"), 0, 0, tiled=True
    )
    guided_total = jnp.sum(gathered[:, 0])
    peak_value = jnp.max(gathered[:, 1])
    entries = img_dev * n_seq * velocity.shape[1]
    guided_norm = jnp.sqrt(guided_total / entries + 1e-06)
    guided = lax.dynamic_slice_in_dim(guided_full, side_index * half_width, half_width, 1)
    latent_next = latent + step_size[0] * guided[None, :, :]
    return (latent_next, jnp.reshape(guided_norm, (1,)), jnp.reshape(peak_value, (1,)))


def solution(mesh):
    n_seq = mesh.shape["seq"]
    n_req = mesh.shape["req"]
    n_x = SEQ_MINOR if n_seq % SEQ_MINOR == 0 else 1
    n_core = CORES if n_req % CORES == 0 else 1
    split_mesh = Mesh(
        mesh.devices.reshape(mesh.shape["cfg"], n_req // n_core, n_core, n_seq // n_x, n_x),
        ("cfg", "ry", "rc", "sz", "sx"),
    )
    req = ("ry", "rc")
    seq = ("sz", "sx")
    in_specs = (
        P("cfg", req, seq, None),
        P(None, "cfg", req, seq, None),
        P("cfg", req, seq, None),
        P("cfg", req),
        P("cfg", req, None),
        P("cfg", req, None),
        P("cfg", req, None),
        P("cfg", req, None),
        P("cfg", req, None),
        P("cfg", req, None),
        P(None, req),
        P(None, req),
        P(req, None),
        P(),
        P(req, seq, "cfg"),
        P(req),
    )
    out_specs = (P(req, seq, "cfg"), P(req), P(req))
    return jax.shard_map(
        per_device, mesh=split_mesh, in_specs=in_specs, out_specs=out_specs, check_vma=False
    )
```

```python
import jax
import jax.numpy as jnp
from jax import lax
from jax.experimental import pallas as pl
from jax.experimental.pallas import tpu as pltpu
from jax.sharding import Mesh, PartitionSpec as P

HEADS = 12
HD = 64
SEQ_MINOR = 4
CORES = 2


guidance_weight = 4.0


def swapped(block, axis, apart):
    count = lax.axis_size(axis)
    route = []
    for low in range(count):
        high = low | 1 << apart
        if high != low and high < count:
            route += [(low, high), (high, low)]
    return lax.ppermute(block, axis, route)


def attention_partials_kernel(q_ref, kv_ref, mask_ref, out_ref):
    rows = q_ref.shape[0]
    lanes = 2 * HD
    lane = lax.broadcasted_iota(jnp.int32, (1, lanes), 1)
    low = lane < HD
    usable = mask_ref[...] > 0
    factor = HD ** (-0.5)
    maxes = []
    sums = []
    for pair in range(HEADS // 2):
        cols = slice(pair * lanes, (pair + 1) * lanes)
        q2 = q_ref[:, cols]
        k2 = kv_ref[0, :, cols]
        v2 = kv_ref[1, :, cols]
        outs = []
        for half in (low, jnp.logical_not(low)):
            q_half = jnp.where(half, q2, jnp.zeros_like(q2))
            logits = lax.dot_general(
                q_half, k2, (((1,), (1,)), ((), ())), preferred_element_type=jnp.float32
            ) * factor
            part_max = jnp.max(jnp.where(usable, logits, -1e30), axis=1, keepdims=True)
            weights = jnp.where(usable, jnp.exp(logits - part_max), 0.0)
            sums.append(jnp.sum(weights, axis=1, keepdims=True))
            maxes.append(part_max)
            outs.append(
                jnp.dot(weights.astype(jnp.bfloat16), v2, preferred_element_type=jnp.float32)
            )
        out_ref[:, cols] = jnp.where(low, outs[0], outs[1])
    width = HEADS * HD
    out_ref[:, width : width + HEADS] = jnp.concatenate(maxes, axis=1)
    out_ref[:, width + HEADS : width + 2 * HEADS] = jnp.concatenate(sums, axis=1)

def attention_partials(q, kv, mask):
    rows = q.shape[0]
    width = HEADS * HD
    return pl.pallas_call(
        attention_partials_kernel,
        out_shape=jax.ShapeDtypeStruct((rows, width + 2 * HEADS), jnp.float32),
        in_specs=[pl.BlockSpec(memory_space=pltpu.VMEM)] * 3,
        out_specs=pl.BlockSpec(memory_space=pltpu.VMEM),
        cost_estimate=pl.CostEstimate(
            flops=8 * rows * kv.shape[1] * width,
            transcendentals=2 * rows * kv.shape[1] * HEADS,
            bytes_accessed=q.size * 2 + kv.size * 2 + rows * (width + 2 * HEADS) * 4,
        ),
    )(q, kv, mask)


def mlp_partials_kernel(x_ref, up_a_ref, up_b_ref, down_a_ref, down_b_ref, out_ref):
    x = x_ref[...]
    inner_a = jax.nn.gelu(
        jnp.dot(x, up_a_ref[...], preferred_element_type=jnp.float32), approximate=True
    ).astype(jnp.bfloat16)
    inner_b = jax.nn.gelu(
        jnp.dot(x, up_b_ref[...], preferred_element_type=jnp.float32), approximate=True
    ).astype(jnp.bfloat16)
    out_ref[...] = (
        jnp.dot(inner_a, down_a_ref[...], preferred_element_type=jnp.float32)
        + jnp.dot(inner_b, down_b_ref[...], preferred_element_type=jnp.float32)
    ).astype(out_ref.dtype)

def mlp_partials(x, up_a, up_b, down_a, down_b):
    rows, width = x.shape
    units = up_a.shape[1]
    return pl.pallas_call(
        mlp_partials_kernel,
        out_shape=jax.ShapeDtypeStruct((rows, down_a.shape[1]), jnp.bfloat16),
        in_specs=[pl.BlockSpec(memory_space=pltpu.VMEM)] * 5,
        out_specs=pl.BlockSpec(memory_space=pltpu.VMEM),
        compiler_params=pltpu.CompilerParams(vmem_limit_bytes=32 * 1024 * 1024),
        cost_estimate=pl.CostEstimate(
            flops=8 * rows * width * units,
            transcendentals=2 * rows * units,
            bytes_accessed=2 * (x.size + 4 * up_a.size + rows * down_a.shape[1]),
        ),
    )(x, up_a, up_b, down_a, down_b)


def modulate_rows(hidden, shift_row, scale_row):
    row_mean = jnp.mean(hidden, axis=1, keepdims=True)
    centered = hidden - row_mean
    row_var = jnp.mean(centered * centered, axis=1, keepdims=True)
    return (
        centered * lax.rsqrt(row_var + 1e-06) * (1.0 + scale_row[None, :]) + shift_row[None, :]
    ).astype(jnp.bfloat16)


def per_device(
    query,
    key_value,
    residual_in,
    text_len,
    attn_gate,
    mlp_shift,
    mlp_scale,
    mlp_gate,
    shift,
    scale,
    w_proj,
    w_up,
    w_down,
    w_out,
    latent,
    step_size,
):
    img_dev = query.shape[2]
    rows_dev = key_value.shape[3]
    txt_dev = rows_dev - img_dev
    length = text_len[0, 0]
    factor = HD ** (-0.5)
    n_x = lax.axis_size("sx")
    x_index = lax.axis_index("sx")
    query_rows = lax.all_to_all(
        jnp.broadcast_to(query[0, 0][None], (n_x,) + query.shape[2:]), "sx", 0, 0, tiled=True
    ).reshape(n_x * img_dev, query.shape[3])
    piece = lax.all_gather(key_value[:, 0, 0], "sz", axis=1, tiled=True)
    q_rows = query_rows.shape[0]
    piece_rows = piece.shape[1]
    positions = jnp.arange(piece_rows, dtype=jnp.int32)
    within = positions % rows_dev
    source = (positions // rows_dev) * n_x + x_index
    text_slot = source * txt_dev + within - img_dev
    usable = ((within < img_dev) | (text_slot < length)).astype(jnp.float32)[None, :]
    width = HEADS * HD
    packed = attention_partials(
        query_rows, piece.reshape(2, piece_rows, width), usable
    ).reshape(n_x, img_dev, width + 2 * HEADS)
    got = lax.all_to_all(packed, "sx", 0, 0, tiled=True)
    got_out = got[:, :, :width].reshape(n_x, img_dev, HEADS, HD)
    got_max = got[:, :, width : width + HEADS]
    got_sum = got[:, :, width + HEADS :]
    row_max = jnp.max(got_max, axis=0)
    rescale = jnp.exp(got_max - row_max[None])
    numerator = jnp.sum(rescale[:, :, :, None] * got_out, axis=0)
    denominator = jnp.sum(rescale * got_sum, axis=0)
    attended = (numerator / denominator[:, :, None]).reshape(img_dev, width).astype(jnp.bfloat16)
    projected = jnp.dot(
        attended,
        lax.all_gather(w_proj, ("ry", "rc"), axis=1, tiled=True),
        preferred_element_type=jnp.float32,
    )
    hidden = residual_in[0, 0].astype(jnp.float32) + attn_gate[0, 0][None, :] * projected
    mlp_in = modulate_rows(hidden, mlp_shift[0, 0], mlp_scale[0, 0])
    n_y = lax.axis_size("ry")
    pair = [(0, 1), (1, 0)]
    up_other = lax.ppermute(w_up, "rc", pair)
    down_other = lax.ppermute(w_down, "rc", pair)
    line_in = lax.all_gather(mlp_in, "ry", axis=0, tiled=True)
    mlp_parts = (
        mlp_partials(line_in, w_up, up_other, w_down, down_other)
        .reshape(n_y, img_dev, w_down.shape[1])
    )
    mlp_out = jnp.sum(
        lax.all_to_all(mlp_parts, "ry", 0, 0, tiled=True).astype(jnp.float32), axis=0
    )
    hidden_two = hidden + mlp_gate[0, 0][None, :] * mlp_out
    modulated = modulate_rows(hidden_two, shift[0, 0], scale[0, 0])
    velocity = jnp.dot(modulated, w_out, preferred_element_type=jnp.float32)
    half_width = velocity.shape[1] // lax.axis_size("cfg")
    side_index = lax.axis_index("cfg")
    received = swapped(velocity, "cfg", 0)
    is_cond = side_index == 0
    cond_part = jnp.where(is_cond, velocity, received)
    uncond = jnp.where(is_cond, received, velocity)
    guided_full = uncond + guidance_weight * (cond_part - uncond)
    partials = jnp.stack([jnp.sum(guided_full * guided_full), jnp.max(jnp.abs(guided_full))])
    n_seq = lax.axis_size(("sz", "sx"))
    gathered = lax.all_to_all(
        jnp.broadcast_to(partials[None], (n_seq, 2)), ("sz", "sx"), 0, 0, tiled=True
    )
    guided_total = jnp.sum(gathered[:, 0])
    peak_value = jnp.max(gathered[:, 1])
    entries = img_dev * n_seq * velocity.shape[1]
    guided_norm = jnp.sqrt(guided_total / entries + 1e-06)
    guided = lax.dynamic_slice_in_dim(guided_full, side_index * half_width, half_width, 1)
    latent_next = latent + step_size[0] * guided[None, :, :]
    return (latent_next, jnp.reshape(guided_norm, (1,)), jnp.reshape(peak_value, (1,)))


def solution(mesh):
    n_seq = mesh.shape["seq"]
    n_req = mesh.shape["req"]
    n_x = SEQ_MINOR if n_seq % SEQ_MINOR == 0 else 1
    n_core = CORES if n_req % CORES == 0 else 1
    split_mesh = Mesh(
        mesh.devices.reshape(mesh.shape["cfg"], n_req // n_core, n_core, n_seq // n_x, n_x),
        ("cfg", "ry", "rc", "sz", "sx"),
    )
    req = ("ry", "rc")
    seq = ("sz", "sx")
    in_specs = (
        P("cfg", req, seq, None),
        P(None, "cfg", req, seq, None),
        P("cfg", req, seq, None),
        P("cfg", req),
        P("cfg", req, None),
        P("cfg", req, None),
        P("cfg", req, None),
        P("cfg", req, None),
        P("cfg", req, None),
        P("cfg", req, None),
        P(None, req),
        P(None, req),
        P(req, None),
        P(),
        P(req, seq, "cfg"),
        P(req),
    )
    out_specs = (P(req, seq, "cfg"), P(req), P(req))
    return jax.shard_map(
        per_device, mesh=split_mesh, in_specs=in_specs, out_specs=out_specs, check_vma=False
    )
```

```python
import jax
import jax.numpy as jnp
from jax import lax
from jax.experimental import pallas as pl
from jax.experimental.pallas import tpu as pltpu
from jax.sharding import Mesh, PartitionSpec as P

HEADS = 12
HD = 64
SEQ_MINOR = 4
CORES = 2


guidance_weight = 4.0


def swapped(block, axis, apart):
    count = lax.axis_size(axis)
    route = []
    for low in range(count):
        high = low | 1 << apart
        if high != low and high < count:
            route += [(low, high), (high, low)]
    return lax.ppermute(block, axis, route)


def attention_partials_kernel(q_ref, kv_ref, mask_ref, out_ref):
    rows = q_ref.shape[0]
    lanes = 2 * HD
    lane = lax.broadcasted_iota(jnp.int32, (1, lanes), 1)
    low = lane < HD
    usable = mask_ref[...] > 0
    factor = HD ** (-0.5)
    maxes = []
    sums = []
    for pair in range(HEADS // 2):
        cols = slice(pair * lanes, (pair + 1) * lanes)
        q2 = q_ref[:, cols]
        k2 = kv_ref[0, :, cols]
        v2 = kv_ref[1, :, cols]
        outs = []
        for half in (low, jnp.logical_not(low)):
            q_half = jnp.where(half, q2, jnp.zeros_like(q2))
            logits = lax.dot_general(
                q_half, k2, (((1,), (1,)), ((), ())), preferred_element_type=jnp.float32
            ) * factor
            part_max = jnp.max(jnp.where(usable, logits, -1e30), axis=1, keepdims=True)
            weights = jnp.where(usable, jnp.exp(logits - part_max), 0.0)
            sums.append(jnp.sum(weights, axis=1, keepdims=True))
            maxes.append(part_max)
            outs.append(
                jnp.dot(weights.astype(jnp.bfloat16), v2, preferred_element_type=jnp.float32)
            )
        out_ref[:, cols] = jnp.where(low, outs[0], outs[1])
    width = HEADS * HD
    out_ref[:, width : width + HEADS] = jnp.concatenate(maxes, axis=1)
    out_ref[:, width + HEADS : width + 2 * HEADS] = jnp.concatenate(sums, axis=1)

def attention_partials(q, kv, mask):
    rows = q.shape[0]
    width = HEADS * HD
    return pl.pallas_call(
        attention_partials_kernel,
        out_shape=jax.ShapeDtypeStruct((rows, width + 2 * HEADS), jnp.float32),
        in_specs=[pl.BlockSpec(memory_space=pltpu.VMEM)] * 3,
        out_specs=pl.BlockSpec(memory_space=pltpu.VMEM),
        cost_estimate=pl.CostEstimate(
            flops=8 * rows * kv.shape[1] * width,
            transcendentals=2 * rows * kv.shape[1] * HEADS,
            bytes_accessed=q.size * 2 + kv.size * 2 + rows * (width + 2 * HEADS) * 4,
        ),
    )(q, kv, mask)


def mlp_partials_kernel(x_ref, up_a_ref, up_b_ref, down_a_ref, down_b_ref, out_ref):
    x = x_ref[...]
    inner_a = jax.nn.gelu(
        jnp.dot(x, up_a_ref[...], preferred_element_type=jnp.float32), approximate=True
    ).astype(jnp.bfloat16)
    inner_b = jax.nn.gelu(
        jnp.dot(x, up_b_ref[...], preferred_element_type=jnp.float32), approximate=True
    ).astype(jnp.bfloat16)
    out_ref[...] = (
        jnp.dot(inner_a, down_a_ref[...], preferred_element_type=jnp.float32)
        + jnp.dot(inner_b, down_b_ref[...], preferred_element_type=jnp.float32)
    ).astype(out_ref.dtype)

def mlp_partials(x, up_a, up_b, down_a, down_b):
    rows, width = x.shape
    units = up_a.shape[1]
    return pl.pallas_call(
        mlp_partials_kernel,
        out_shape=jax.ShapeDtypeStruct((rows, down_a.shape[1]), jnp.bfloat16),
        in_specs=[pl.BlockSpec(memory_space=pltpu.VMEM)] * 5,
        out_specs=pl.BlockSpec(memory_space=pltpu.VMEM),
        compiler_params=pltpu.CompilerParams(vmem_limit_bytes=32 * 1024 * 1024),
        cost_estimate=pl.CostEstimate(
            flops=8 * rows * width * units,
            transcendentals=2 * rows * units,
            bytes_accessed=2 * (x.size + 4 * up_a.size + rows * down_a.shape[1]),
        ),
    )(x, up_a, up_b, down_a, down_b)


def modulate_rows(hidden, shift_row, scale_row):
    row_mean = jnp.mean(hidden, axis=1, keepdims=True)
    centered = hidden - row_mean
    row_var = jnp.mean(centered * centered, axis=1, keepdims=True)
    return (
        centered * lax.rsqrt(row_var + 1e-06) * (1.0 + scale_row[None, :]) + shift_row[None, :]
    ).astype(jnp.bfloat16)


def per_device(
    query,
    key_value,
    residual_in,
    text_len,
    attn_gate,
    mlp_shift,
    mlp_scale,
    mlp_gate,
    shift,
    scale,
    w_proj,
    w_up,
    w_down,
    w_out,
    latent,
    step_size,
):
    img_dev = query.shape[2]
    rows_dev = key_value.shape[3]
    txt_dev = rows_dev - img_dev
    length = text_len[0, 0]
    factor = HD ** (-0.5)
    n_x = lax.axis_size("sx")
    x_index = lax.axis_index("sx")
    query_rows = lax.all_to_all(
        jnp.broadcast_to(query[0, 0][None], (n_x,) + query.shape[2:]), "sx", 0, 0, tiled=True
    ).reshape(n_x * img_dev, query.shape[3])
    piece = lax.all_gather(key_value[:, 0, 0], "sz", axis=1, tiled=True)
    q_rows = query_rows.shape[0]
    piece_rows = piece.shape[1]
    positions = jnp.arange(piece_rows, dtype=jnp.int32)
    within = positions % rows_dev
    source = (positions // rows_dev) * n_x + x_index
    text_slot = source * txt_dev + within - img_dev
    usable = ((within < img_dev) | (text_slot < length)).astype(jnp.float32)[None, :]
    width = HEADS * HD
    packed = attention_partials(
        query_rows, piece.reshape(2, piece_rows, width), usable
    ).reshape(n_x, img_dev, width + 2 * HEADS)
    got = lax.all_to_all(packed, "sx", 0, 0, tiled=True)
    got_out = got[:, :, :width].reshape(n_x, img_dev, HEADS, HD)
    got_max = got[:, :, width : width + HEADS]
    got_sum = got[:, :, width + HEADS :]
    row_max = jnp.max(got_max, axis=0)
    rescale = jnp.exp(got_max - row_max[None])
    numerator = jnp.einsum(
        "iqh,iqhd->qhd", rescale, got_out, precision=lax.Precision.HIGHEST
    )
    denominator = jnp.sum(rescale * got_sum, axis=0)
    attended = (numerator / denominator[:, :, None]).reshape(img_dev, width).astype(jnp.bfloat16)
    projected = jnp.dot(
        attended,
        lax.all_gather(w_proj, ("ry", "rc"), axis=1, tiled=True),
        preferred_element_type=jnp.float32,
    )
    hidden = residual_in[0, 0].astype(jnp.float32) + attn_gate[0, 0][None, :] * projected
    mlp_in = modulate_rows(hidden, mlp_shift[0, 0], mlp_scale[0, 0])
    n_y = lax.axis_size("ry")
    pair = [(0, 1), (1, 0)]
    up_other = lax.ppermute(w_up, "rc", pair)
    down_other = lax.ppermute(w_down, "rc", pair)
    line_in = lax.all_gather(mlp_in, "ry", axis=0, tiled=True)
    mlp_parts = (
        mlp_partials(line_in, w_up, up_other, w_down, down_other)
        .reshape(n_y, img_dev, w_down.shape[1])
    )
    mlp_out = jnp.sum(
        lax.all_to_all(mlp_parts, "ry", 0, 0, tiled=True).astype(jnp.float32), axis=0
    )
    hidden_two = hidden + mlp_gate[0, 0][None, :] * mlp_out
    modulated = modulate_rows(hidden_two, shift[0, 0], scale[0, 0])
    velocity = jnp.dot(modulated, w_out, preferred_element_type=jnp.float32)
    half_width = velocity.shape[1] // lax.axis_size("cfg")
    side_index = lax.axis_index("cfg")
    received = swapped(velocity, "cfg", 0)
    is_cond = side_index == 0
    cond_part = jnp.where(is_cond, velocity, received)
    uncond = jnp.where(is_cond, received, velocity)
    guided_full = uncond + guidance_weight * (cond_part - uncond)
    partials = jnp.stack([jnp.sum(guided_full * guided_full), jnp.max(jnp.abs(guided_full))])
    n_seq = lax.axis_size(("sz", "sx"))
    gathered = lax.all_to_all(
        jnp.broadcast_to(partials[None], (n_seq, 2)), ("sz", "sx"), 0, 0, tiled=True
    )
    guided_total = jnp.sum(gathered[:, 0])
    peak_value = jnp.max(gathered[:, 1])
    entries = img_dev * n_seq * velocity.shape[1]
    guided_norm = jnp.sqrt(guided_total / entries + 1e-06)
    guided = lax.dynamic_slice_in_dim(guided_full, side_index * half_width, half_width, 1)
    latent_next = latent + step_size[0] * guided[None, :, :]
    return (latent_next, jnp.reshape(guided_norm, (1,)), jnp.reshape(peak_value, (1,)))


def solution(mesh):
    n_seq = mesh.shape["seq"]
    n_req = mesh.shape["req"]
    n_x = SEQ_MINOR if n_seq % SEQ_MINOR == 0 else 1
    n_core = CORES if n_req % CORES == 0 else 1
    split_mesh = Mesh(
        mesh.devices.reshape(mesh.shape["cfg"], n_req // n_core, n_core, n_seq // n_x, n_x),
        ("cfg", "ry", "rc", "sz", "sx"),
    )
    req = ("ry", "rc")
    seq = ("sz", "sx")
    in_specs = (
        P("cfg", req, seq, None),
        P(None, "cfg", req, seq, None),
        P("cfg", req, seq, None),
        P("cfg", req),
        P("cfg", req, None),
        P("cfg", req, None),
        P("cfg", req, None),
        P("cfg", req, None),
        P("cfg", req, None),
        P("cfg", req, None),
        P(None, req),
        P(None, req),
        P(req, None),
        P(),
        P(req, seq, "cfg"),
        P(req),
    )
    out_specs = (P(req, seq, "cfg"), P(req), P(req))
    return jax.shard_map(
        per_device, mesh=split_mesh, in_specs=in_specs, out_specs=out_specs, check_vma=False
    )
```

```python
import jax
import jax.numpy as jnp
from jax import lax
from jax.experimental import pallas as pl
from jax.experimental.pallas import tpu as pltpu
from jax.sharding import Mesh, PartitionSpec as P

HEADS = 12
HD = 64
SEQ_MINOR = 4
CORES = 2


guidance_weight = 4.0


def swapped(block, axis, apart):
    count = lax.axis_size(axis)
    route = []
    for low in range(count):
        high = low | 1 << apart
        if high != low and high < count:
            route += [(low, high), (high, low)]
    return lax.ppermute(block, axis, route)


def attention_partials_kernel(q_ref, kv_ref, mask_ref, out_ref):
    rows = q_ref.shape[0]
    lanes = 2 * HD
    lane = lax.broadcasted_iota(jnp.int32, (1, lanes), 1)
    low = lane < HD
    usable = mask_ref[...] > 0
    factor = HD ** (-0.5)
    maxes = []
    sums = []
    for pair in range(HEADS // 2):
        cols = slice(pair * lanes, (pair + 1) * lanes)
        q2 = q_ref[:, cols]
        k2 = kv_ref[0, :, cols]
        v2 = kv_ref[1, :, cols]
        outs = []
        for half in (low, jnp.logical_not(low)):
            q_half = jnp.where(half, q2, jnp.zeros_like(q2))
            logits = lax.dot_general(
                q_half, k2, (((1,), (1,)), ((), ())), preferred_element_type=jnp.float32
            ) * factor
            part_max = jnp.max(jnp.where(usable, logits, -1e30), axis=1, keepdims=True)
            weights = jnp.where(usable, jnp.exp(logits - part_max), 0.0)
            sums.append(jnp.sum(weights, axis=1, keepdims=True))
            maxes.append(part_max)
            outs.append(
                jnp.dot(weights.astype(jnp.bfloat16), v2, preferred_element_type=jnp.float32)
            )
        out_ref[:, cols] = jnp.where(low, outs[0], outs[1])
    width = HEADS * HD
    out_ref[:, width : width + HEADS] = jnp.concatenate(maxes, axis=1)
    out_ref[:, width + HEADS : width + 2 * HEADS] = jnp.concatenate(sums, axis=1)

def attention_partials(q, kv, mask):
    rows = q.shape[0]
    width = HEADS * HD
    return pl.pallas_call(
        attention_partials_kernel,
        out_shape=jax.ShapeDtypeStruct((rows, width + 2 * HEADS), jnp.float32),
        in_specs=[pl.BlockSpec(memory_space=pltpu.VMEM)] * 3,
        out_specs=pl.BlockSpec(memory_space=pltpu.VMEM),
        cost_estimate=pl.CostEstimate(
            flops=8 * rows * kv.shape[1] * width,
            transcendentals=2 * rows * kv.shape[1] * HEADS,
            bytes_accessed=q.size * 2 + kv.size * 2 + rows * (width + 2 * HEADS) * 4,
        ),
    )(q, kv, mask)


def modulate_rows(hidden, shift_row, scale_row):
    row_mean = jnp.mean(hidden, axis=1, keepdims=True)
    centered = hidden - row_mean
    row_var = jnp.mean(centered * centered, axis=1, keepdims=True)
    return (
        centered * lax.rsqrt(row_var + 1e-06) * (1.0 + scale_row[None, :]) + shift_row[None, :]
    ).astype(jnp.bfloat16)


def per_device(
    query,
    key_value,
    residual_in,
    text_len,
    attn_gate,
    mlp_shift,
    mlp_scale,
    mlp_gate,
    shift,
    scale,
    w_proj,
    w_up,
    w_down,
    w_out,
    latent,
    step_size,
):
    img_dev = query.shape[2]
    rows_dev = key_value.shape[3]
    txt_dev = rows_dev - img_dev
    length = text_len[0, 0]
    factor = HD ** (-0.5)
    n_x = lax.axis_size("sx")
    x_index = lax.axis_index("sx")
    n_z = lax.axis_size("sz")
    kv_blocks = lax.all_to_all(
        jnp.broadcast_to(key_value[:, 0, 0][None], (n_z,) + key_value[:, 0, 0].shape),
        "sz",
        0,
        0,
        tiled=True,
    )
    query_rows = lax.all_gather(query[0, 0], "sx", axis=0, tiled=True)
    piece = jnp.swapaxes(kv_blocks, 0, 1).reshape(
        2, n_z * rows_dev, key_value.shape[4]
    )
    q_rows = query_rows.shape[0]
    piece_rows = piece.shape[1]
    positions = jnp.arange(piece_rows, dtype=jnp.int32)
    within = positions % rows_dev
    source = (positions // rows_dev) * n_x + x_index
    text_slot = source * txt_dev + within - img_dev
    usable = ((within < img_dev) | (text_slot < length)).astype(jnp.float32)[None, :]
    width = HEADS * HD
    packed = attention_partials(
        query_rows, piece.reshape(2, piece_rows, width), usable
    ).reshape(n_x, img_dev, width + 2 * HEADS)
    got = lax.all_to_all(packed, "sx", 0, 0, tiled=True)
    got_out = got[:, :, :width].reshape(n_x, img_dev, HEADS, HD)
    got_max = got[:, :, width : width + HEADS]
    got_sum = got[:, :, width + HEADS :]
    row_max = jnp.max(got_max, axis=0)
    rescale = jnp.exp(got_max - row_max[None])
    numerator = jnp.sum(rescale[:, :, :, None] * got_out, axis=0)
    denominator = jnp.sum(rescale * got_sum, axis=0)
    attended = (numerator / denominator[:, :, None]).reshape(img_dev, width).astype(jnp.bfloat16)
    projected = jnp.dot(
        attended,
        lax.all_gather(w_proj, ("ry", "rc"), axis=1, tiled=True),
        preferred_element_type=jnp.float32,
    )
    hidden = residual_in[0, 0].astype(jnp.float32) + attn_gate[0, 0][None, :] * projected
    mlp_in = modulate_rows(hidden, mlp_shift[0, 0], mlp_scale[0, 0])
    n_y = lax.axis_size("ry")
    pair = [(0, 1), (1, 0)]
    up_other = lax.ppermute(w_up, "rc", pair)
    down_other = lax.ppermute(w_down, "rc", pair)
    line_in = lax.all_gather(mlp_in, "ry", axis=0, tiled=True)
    inner_own = jax.nn.gelu(
        jnp.dot(line_in, w_up, preferred_element_type=jnp.float32), approximate=True
    ).astype(jnp.bfloat16)
    inner_other = jax.nn.gelu(
        jnp.dot(line_in, up_other, preferred_element_type=jnp.float32), approximate=True
    ).astype(jnp.bfloat16)
    mlp_parts = (
        (
            jnp.dot(inner_own, w_down, preferred_element_type=jnp.float32)
            + jnp.dot(inner_other, down_other, preferred_element_type=jnp.float32)
        )
        .astype(jnp.bfloat16)
        .reshape(n_y, img_dev, w_down.shape[1])
    )
    mlp_out = jnp.sum(
        lax.all_to_all(mlp_parts, "ry", 0, 0, tiled=True).astype(jnp.float32), axis=0
    )
    hidden_two = hidden + mlp_gate[0, 0][None, :] * mlp_out
    modulated = modulate_rows(hidden_two, shift[0, 0], scale[0, 0])
    velocity = jnp.dot(modulated, w_out, preferred_element_type=jnp.float32)
    half_width = velocity.shape[1] // lax.axis_size("cfg")
    side_index = lax.axis_index("cfg")
    received = swapped(velocity, "cfg", 0)
    is_cond = side_index == 0
    cond_part = jnp.where(is_cond, velocity, received)
    uncond = jnp.where(is_cond, received, velocity)
    guided_full = uncond + guidance_weight * (cond_part - uncond)
    partials = jnp.stack([jnp.sum(guided_full * guided_full), jnp.max(jnp.abs(guided_full))])
    n_seq = lax.axis_size(("sz", "sx"))
    gathered = lax.all_to_all(
        jnp.broadcast_to(partials[None], (n_seq, 2)), ("sz", "sx"), 0, 0, tiled=True
    )
    guided_total = jnp.sum(gathered[:, 0])
    peak_value = jnp.max(gathered[:, 1])
    entries = img_dev * n_seq * velocity.shape[1]
    guided_norm = jnp.sqrt(guided_total / entries + 1e-06)
    guided = lax.dynamic_slice_in_dim(guided_full, side_index * half_width, half_width, 1)
    latent_next = latent + step_size[0] * guided[None, :, :]
    return (latent_next, jnp.reshape(guided_norm, (1,)), jnp.reshape(peak_value, (1,)))


def solution(mesh):
    n_seq = mesh.shape["seq"]
    n_req = mesh.shape["req"]
    n_x = SEQ_MINOR if n_seq % SEQ_MINOR == 0 else 1
    n_core = CORES if n_req % CORES == 0 else 1
    split_mesh = Mesh(
        mesh.devices.reshape(mesh.shape["cfg"], n_req // n_core, n_core, n_seq // n_x, n_x),
        ("cfg", "ry", "rc", "sz", "sx"),
    )
    req = ("ry", "rc")
    seq = ("sz", "sx")
    in_specs = (
        P("cfg", req, seq, None),
        P(None, "cfg", req, seq, None),
        P("cfg", req, seq, None),
        P("cfg", req),
        P("cfg", req, None),
        P("cfg", req, None),
        P("cfg", req, None),
        P("cfg", req, None),
        P("cfg", req, None),
        P("cfg", req, None),
        P(None, req),
        P(None, req),
        P(req, None),
        P(),
        P(req, seq, "cfg"),
        P(req),
    )
    out_specs = (P(req, seq, "cfg"), P(req), P(req))
    return jax.shard_map(
        per_device, mesh=split_mesh, in_specs=in_specs, out_specs=out_specs, check_vma=False
    )
```

```python
import jax
import jax.numpy as jnp
from jax import lax
from jax.experimental import pallas as pl
from jax.experimental.pallas import tpu as pltpu
from jax.sharding import Mesh, PartitionSpec as P

HEADS = 12
HD = 64
SEQ_MINOR = 4
CORES = 2


guidance_weight = 4.0


def swapped(block, axis, apart):
    count = lax.axis_size(axis)
    route = []
    for low in range(count):
        high = low | 1 << apart
        if high != low and high < count:
            route += [(low, high), (high, low)]
    return lax.ppermute(block, axis, route)


def attention_partials_kernel(q_ref, kv_ref, mask_ref, out_ref):
    rows = q_ref.shape[0]
    lanes = 2 * HD
    lane = lax.broadcasted_iota(jnp.int32, (1, lanes), 1)
    low = lane < HD
    usable = mask_ref[...] > 0
    factor = HD ** (-0.5)
    maxes = []
    sums = []
    for pair in range(HEADS // 2):
        cols = slice(pair * lanes, (pair + 1) * lanes)
        q2 = q_ref[:, cols]
        k2 = jnp.concatenate([kv_ref[z, 0, :, cols] for z in range(kv_ref.shape[0])], axis=0)
        v2 = jnp.concatenate([kv_ref[z, 1, :, cols] for z in range(kv_ref.shape[0])], axis=0)
        outs = []
        for half in (low, jnp.logical_not(low)):
            q_half = jnp.where(half, q2, jnp.zeros_like(q2))
            logits = lax.dot_general(
                q_half, k2, (((1,), (1,)), ((), ())), preferred_element_type=jnp.float32
            ) * factor
            part_max = jnp.max(jnp.where(usable, logits, -1e30), axis=1, keepdims=True)
            weights = jnp.where(usable, jnp.exp(logits - part_max), 0.0)
            sums.append(jnp.sum(weights, axis=1, keepdims=True))
            maxes.append(part_max)
            outs.append(
                jnp.dot(weights.astype(jnp.bfloat16), v2, preferred_element_type=jnp.float32)
            )
        out_ref[:, cols] = jnp.where(low, outs[0], outs[1])
    width = HEADS * HD
    out_ref[:, width : width + HEADS] = jnp.concatenate(maxes, axis=1)
    out_ref[:, width + HEADS : width + 2 * HEADS] = jnp.concatenate(sums, axis=1)

def attention_partials(q, kv, mask):
    rows = q.shape[0]
    width = HEADS * HD
    return pl.pallas_call(
        attention_partials_kernel,
        out_shape=jax.ShapeDtypeStruct((rows, width + 2 * HEADS), jnp.float32),
        in_specs=[pl.BlockSpec(memory_space=pltpu.VMEM)] * 3,
        out_specs=pl.BlockSpec(memory_space=pltpu.VMEM),
        cost_estimate=pl.CostEstimate(
            flops=8 * rows * kv.shape[0] * kv.shape[2] * width,
            transcendentals=2 * rows * kv.shape[0] * kv.shape[2] * HEADS,
            bytes_accessed=q.size * 2 + kv.size * 2 + rows * (width + 2 * HEADS) * 4,
        ),
    )(q, kv, mask)


def modulate_rows(hidden, shift_row, scale_row):
    row_mean = jnp.mean(hidden, axis=1, keepdims=True)
    centered = hidden - row_mean
    row_var = jnp.mean(centered * centered, axis=1, keepdims=True)
    return (
        centered * lax.rsqrt(row_var + 1e-06) * (1.0 + scale_row[None, :]) + shift_row[None, :]
    ).astype(jnp.bfloat16)


def per_device(
    query,
    key_value,
    residual_in,
    text_len,
    attn_gate,
    mlp_shift,
    mlp_scale,
    mlp_gate,
    shift,
    scale,
    w_proj,
    w_up,
    w_down,
    w_out,
    latent,
    step_size,
):
    img_dev = query.shape[2]
    rows_dev = key_value.shape[3]
    txt_dev = rows_dev - img_dev
    length = text_len[0, 0]
    factor = HD ** (-0.5)
    n_x = lax.axis_size("sx")
    x_index = lax.axis_index("sx")
    n_z = lax.axis_size("sz")
    kv_blocks = lax.all_to_all(
        jnp.broadcast_to(key_value[:, 0, 0][None], (n_z,) + key_value[:, 0, 0].shape),
        "sz",
        0,
        0,
        tiled=True,
    )
    query_rows = lax.all_gather(query[0, 0], "sx", axis=0, tiled=True)
    q_rows = query_rows.shape[0]
    piece_rows = n_z * rows_dev
    positions = jnp.arange(piece_rows, dtype=jnp.int32)
    within = positions % rows_dev
    source = (positions // rows_dev) * n_x + x_index
    text_slot = source * txt_dev + within - img_dev
    usable = ((within < img_dev) | (text_slot < length)).astype(jnp.float32)[None, :]
    width = HEADS * HD
    packed = attention_partials(
        query_rows, kv_blocks, usable
    ).reshape(n_x, img_dev, width + 2 * HEADS)
    got = lax.all_to_all(packed, "sx", 0, 0, tiled=True)
    got_out = got[:, :, :width].reshape(n_x, img_dev, HEADS, HD)
    got_max = got[:, :, width : width + HEADS]
    got_sum = got[:, :, width + HEADS :]
    row_max = jnp.max(got_max, axis=0)
    rescale = jnp.exp(got_max - row_max[None])
    numerator = jnp.sum(rescale[:, :, :, None] * got_out, axis=0)
    denominator = jnp.sum(rescale * got_sum, axis=0)
    attended = (numerator / denominator[:, :, None]).reshape(img_dev, width).astype(jnp.bfloat16)
    projected = jnp.dot(
        attended,
        lax.all_gather(w_proj, ("ry", "rc"), axis=1, tiled=True),
        preferred_element_type=jnp.float32,
    )
    hidden = residual_in[0, 0].astype(jnp.float32) + attn_gate[0, 0][None, :] * projected
    mlp_in = modulate_rows(hidden, mlp_shift[0, 0], mlp_scale[0, 0])
    n_y = lax.axis_size("ry")
    pair = [(0, 1), (1, 0)]
    up_other = lax.ppermute(w_up, "rc", pair)
    down_other = lax.ppermute(w_down, "rc", pair)
    line_in = lax.all_gather(mlp_in, "ry", axis=0, tiled=True)
    inner_own = jax.nn.gelu(
        jnp.dot(line_in, w_up, preferred_element_type=jnp.float32), approximate=True
    ).astype(jnp.bfloat16)
    inner_other = jax.nn.gelu(
        jnp.dot(line_in, up_other, preferred_element_type=jnp.float32), approximate=True
    ).astype(jnp.bfloat16)
    mlp_parts = (
        (
            jnp.dot(inner_own, w_down, preferred_element_type=jnp.float32)
            + jnp.dot(inner_other, down_other, preferred_element_type=jnp.float32)
        )
        .astype(jnp.bfloat16)
        .reshape(n_y, img_dev, w_down.shape[1])
    )
    mlp_out = jnp.sum(
        lax.all_to_all(mlp_parts, "ry", 0, 0, tiled=True).astype(jnp.float32), axis=0
    )
    hidden_two = hidden + mlp_gate[0, 0][None, :] * mlp_out
    modulated = modulate_rows(hidden_two, shift[0, 0], scale[0, 0])
    velocity = jnp.dot(modulated, w_out, preferred_element_type=jnp.float32)
    half_width = velocity.shape[1] // lax.axis_size("cfg")
    side_index = lax.axis_index("cfg")
    received = swapped(velocity, "cfg", 0)
    is_cond = side_index == 0
    cond_part = jnp.where(is_cond, velocity, received)
    uncond = jnp.where(is_cond, received, velocity)
    guided_full = uncond + guidance_weight * (cond_part - uncond)
    partials = jnp.stack([jnp.sum(guided_full * guided_full), jnp.max(jnp.abs(guided_full))])
    n_seq = lax.axis_size(("sz", "sx"))
    gathered = lax.all_to_all(
        jnp.broadcast_to(partials[None], (n_seq, 2)), ("sz", "sx"), 0, 0, tiled=True
    )
    guided_total = jnp.sum(gathered[:, 0])
    peak_value = jnp.max(gathered[:, 1])
    entries = img_dev * n_seq * velocity.shape[1]
    guided_norm = jnp.sqrt(guided_total / entries + 1e-06)
    guided = lax.dynamic_slice_in_dim(guided_full, side_index * half_width, half_width, 1)
    latent_next = latent + step_size[0] * guided[None, :, :]
    return (latent_next, jnp.reshape(guided_norm, (1,)), jnp.reshape(peak_value, (1,)))


def solution(mesh):
    n_seq = mesh.shape["seq"]
    n_req = mesh.shape["req"]
    n_x = SEQ_MINOR if n_seq % SEQ_MINOR == 0 else 1
    n_core = CORES if n_req % CORES == 0 else 1
    split_mesh = Mesh(
        mesh.devices.reshape(mesh.shape["cfg"], n_req // n_core, n_core, n_seq // n_x, n_x),
        ("cfg", "ry", "rc", "sz", "sx"),
    )
    req = ("ry", "rc")
    seq = ("sz", "sx")
    in_specs = (
        P("cfg", req, seq, None),
        P(None, "cfg", req, seq, None),
        P("cfg", req, seq, None),
        P("cfg", req),
        P("cfg", req, None),
        P("cfg", req, None),
        P("cfg", req, None),
        P("cfg", req, None),
        P("cfg", req, None),
        P("cfg", req, None),
        P(None, req),
        P(None, req),
        P(req, None),
        P(),
        P(req, seq, "cfg"),
        P(req),
    )
    out_specs = (P(req, seq, "cfg"), P(req), P(req))
    return jax.shard_map(
        per_device, mesh=split_mesh, in_specs=in_specs, out_specs=out_specs, check_vma=False
    )
```

```python
import jax
import jax.numpy as jnp
from jax import lax
from jax.experimental import pallas as pl
from jax.experimental.pallas import tpu as pltpu
from jax.sharding import Mesh, PartitionSpec as P

HEADS = 12
HD = 64
SEQ_MINOR = 4
CORES = 2


guidance_weight = 4.0


def swapped(block, axis, apart):
    count = lax.axis_size(axis)
    route = []
    for low in range(count):
        high = low | 1 << apart
        if high != low and high < count:
            route += [(low, high), (high, low)]
    return lax.ppermute(block, axis, route)


def attention_partials_kernel(q_ref, kv_ref, mask_ref, out_ref):
    rows = q_ref.shape[0]
    lanes = 2 * HD
    lane = lax.broadcasted_iota(jnp.int32, (1, lanes), 1)
    low = lane < HD
    usable = mask_ref[...] > 0
    factor = HD ** (-0.5)
    maxes = []
    sums = []
    for pair in range(HEADS // 2):
        cols = slice(pair * lanes, (pair + 1) * lanes)
        q2 = q_ref[:, cols]
        k2 = jnp.concatenate([kv_ref[z, 0, :, cols] for z in range(kv_ref.shape[0])], axis=0)
        v2 = jnp.concatenate([kv_ref[z, 1, :, cols] for z in range(kv_ref.shape[0])], axis=0)
        outs = []
        for half in (low, jnp.logical_not(low)):
            q_half = jnp.where(half, q2, jnp.zeros_like(q2))
            logits = lax.dot_general(
                q_half, k2, (((1,), (1,)), ((), ())), preferred_element_type=jnp.float32
            ) * factor
            part_max = jnp.max(jnp.where(usable, logits, -1e30), axis=1, keepdims=True)
            weights = jnp.where(usable, jnp.exp(logits - part_max), 0.0)
            sums.append(jnp.sum(weights, axis=1, keepdims=True))
            maxes.append(part_max)
            outs.append(
                jnp.dot(weights.astype(jnp.bfloat16), v2, preferred_element_type=jnp.float32)
            )
        out_ref[:, cols] = jnp.where(low, outs[0], outs[1])
    width = HEADS * HD
    out_ref[:, width : width + HEADS] = jnp.concatenate(maxes, axis=1)
    out_ref[:, width + HEADS : width + 2 * HEADS] = jnp.concatenate(sums, axis=1)

def attention_partials(q, kv, mask):
    rows = q.shape[0]
    width = HEADS * HD
    return pl.pallas_call(
        attention_partials_kernel,
        out_shape=jax.ShapeDtypeStruct((rows, width + 2 * HEADS), jnp.float32),
        in_specs=[pl.BlockSpec(memory_space=pltpu.VMEM)] * 3,
        out_specs=pl.BlockSpec(memory_space=pltpu.VMEM),
        cost_estimate=pl.CostEstimate(
            flops=8 * rows * kv.shape[0] * kv.shape[2] * width,
            transcendentals=2 * rows * kv.shape[0] * kv.shape[2] * HEADS,
            bytes_accessed=q.size * 2 + kv.size * 2 + rows * (width + 2 * HEADS) * 4,
        ),
    )(q, kv, mask)


def mlp_partials_kernel(x_ref, up_a_ref, up_b_ref, down_a_ref, down_b_ref, out_ref):
    x = x_ref[...]
    inner_a = jax.nn.gelu(
        jnp.dot(x, up_a_ref[...], preferred_element_type=jnp.float32), approximate=True
    ).astype(jnp.bfloat16)
    inner_b = jax.nn.gelu(
        jnp.dot(x, up_b_ref[...], preferred_element_type=jnp.float32), approximate=True
    ).astype(jnp.bfloat16)
    out_ref[...] = (
        jnp.dot(inner_a, down_a_ref[...], preferred_element_type=jnp.float32)
        + jnp.dot(inner_b, down_b_ref[...], preferred_element_type=jnp.float32)
    ).astype(out_ref.dtype)

def mlp_partials(x, up_a, up_b, down_a, down_b):
    rows, width = x.shape
    units = up_a.shape[1]
    return pl.pallas_call(
        mlp_partials_kernel,
        out_shape=jax.ShapeDtypeStruct((rows, down_a.shape[1]), jnp.bfloat16),
        in_specs=[pl.BlockSpec(memory_space=pltpu.VMEM)] * 5,
        out_specs=pl.BlockSpec(memory_space=pltpu.VMEM),
        compiler_params=pltpu.CompilerParams(vmem_limit_bytes=32 * 1024 * 1024),
        cost_estimate=pl.CostEstimate(
            flops=8 * rows * width * units,
            transcendentals=2 * rows * units,
            bytes_accessed=2 * (x.size + 4 * up_a.size + rows * down_a.shape[1]),
        ),
    )(x, up_a, up_b, down_a, down_b)


def modulate_rows(hidden, shift_row, scale_row):
    row_mean = jnp.mean(hidden, axis=1, keepdims=True)
    centered = hidden - row_mean
    row_var = jnp.mean(centered * centered, axis=1, keepdims=True)
    return (
        centered * lax.rsqrt(row_var + 1e-06) * (1.0 + scale_row[None, :]) + shift_row[None, :]
    ).astype(jnp.bfloat16)


def per_device(
    query,
    key_value,
    residual_in,
    text_len,
    attn_gate,
    mlp_shift,
    mlp_scale,
    mlp_gate,
    shift,
    scale,
    w_proj,
    w_up,
    w_down,
    w_out,
    latent,
    step_size,
):
    img_dev = query.shape[2]
    rows_dev = key_value.shape[3]
    txt_dev = rows_dev - img_dev
    length = text_len[0, 0]
    factor = HD ** (-0.5)
    n_x = lax.axis_size("sx")
    x_index = lax.axis_index("sx")
    n_z = lax.axis_size("sz")
    kv_blocks = lax.all_to_all(
        jnp.broadcast_to(key_value[:, 0, 0][None], (n_z,) + key_value[:, 0, 0].shape),
        "sz",
        0,
        0,
        tiled=True,
    )
    query_rows = lax.all_gather(query[0, 0], "sx", axis=0, tiled=True)
    q_rows = query_rows.shape[0]
    piece_rows = n_z * rows_dev
    positions = jnp.arange(piece_rows, dtype=jnp.int32)
    within = positions % rows_dev
    source = (positions // rows_dev) * n_x + x_index
    text_slot = source * txt_dev + within - img_dev
    usable = ((within < img_dev) | (text_slot < length)).astype(jnp.float32)[None, :]
    width = HEADS * HD
    packed = attention_partials(
        query_rows, kv_blocks, usable
    ).reshape(n_x, img_dev, width + 2 * HEADS)
    got = lax.all_to_all(packed, "sx", 0, 0, tiled=True)
    got_out = got[:, :, :width].reshape(n_x, img_dev, HEADS, HD)
    got_max = got[:, :, width : width + HEADS]
    got_sum = got[:, :, width + HEADS :]
    row_max = jnp.max(got_max, axis=0)
    rescale = jnp.exp(got_max - row_max[None])
    numerator = jnp.sum(rescale[:, :, :, None] * got_out, axis=0)
    denominator = jnp.sum(rescale * got_sum, axis=0)
    attended = (numerator / denominator[:, :, None]).reshape(img_dev, width).astype(jnp.bfloat16)
    projected = jnp.dot(
        attended,
        lax.all_gather(w_proj, ("ry", "rc"), axis=1, tiled=True),
        preferred_element_type=jnp.float32,
    )
    hidden = residual_in[0, 0].astype(jnp.float32) + attn_gate[0, 0][None, :] * projected
    mlp_in = modulate_rows(hidden, mlp_shift[0, 0], mlp_scale[0, 0])
    n_y = lax.axis_size("ry")
    pair = [(0, 1), (1, 0)]
    up_other = lax.ppermute(w_up, "rc", pair)
    down_other = lax.ppermute(w_down, "rc", pair)
    line_in = lax.all_gather(mlp_in, "ry", axis=0, tiled=True)
    mlp_parts = (
        mlp_partials(line_in, w_up, up_other, w_down, down_other)
        .reshape(n_y, img_dev, w_down.shape[1])
    )
    mlp_out = jnp.sum(
        lax.all_to_all(mlp_parts, "ry", 0, 0, tiled=True).astype(jnp.float32), axis=0
    )
    hidden_two = hidden + mlp_gate[0, 0][None, :] * mlp_out
    modulated = modulate_rows(hidden_two, shift[0, 0], scale[0, 0])
    velocity = jnp.dot(modulated, w_out, preferred_element_type=jnp.float32)
    half_width = velocity.shape[1] // lax.axis_size("cfg")
    side_index = lax.axis_index("cfg")
    received = swapped(velocity, "cfg", 0)
    is_cond = side_index == 0
    cond_part = jnp.where(is_cond, velocity, received)
    uncond = jnp.where(is_cond, received, velocity)
    guided_full = uncond + guidance_weight * (cond_part - uncond)
    partials = jnp.stack([jnp.sum(guided_full * guided_full), jnp.max(jnp.abs(guided_full))])
    n_seq = lax.axis_size(("sz", "sx"))
    gathered = lax.all_to_all(
        jnp.broadcast_to(partials[None], (n_seq, 2)), ("sz", "sx"), 0, 0, tiled=True
    )
    guided_total = jnp.sum(gathered[:, 0])
    peak_value = jnp.max(gathered[:, 1])
    entries = img_dev * n_seq * velocity.shape[1]
    guided_norm = jnp.sqrt(guided_total / entries + 1e-06)
    guided = lax.dynamic_slice_in_dim(guided_full, side_index * half_width, half_width, 1)
    latent_next = latent + step_size[0] * guided[None, :, :]
    return (latent_next, jnp.reshape(guided_norm, (1,)), jnp.reshape(peak_value, (1,)))


def solution(mesh):
    n_seq = mesh.shape["seq"]
    n_req = mesh.shape["req"]
    n_x = SEQ_MINOR if n_seq % SEQ_MINOR == 0 else 1
    n_core = CORES if n_req % CORES == 0 else 1
    split_mesh = Mesh(
        mesh.devices.reshape(mesh.shape["cfg"], n_req // n_core, n_core, n_seq // n_x, n_x),
        ("cfg", "ry", "rc", "sz", "sx"),
    )
    req = ("ry", "rc")
    seq = ("sz", "sx")
    in_specs = (
        P("cfg", req, seq, None),
        P(None, "cfg", req, seq, None),
        P("cfg", req, seq, None),
        P("cfg", req),
        P("cfg", req, None),
        P("cfg", req, None),
        P("cfg", req, None),
        P("cfg", req, None),
        P("cfg", req, None),
        P("cfg", req, None),
        P(None, req),
        P(None, req),
        P(req, None),
        P(),
        P(req, seq, "cfg"),
        P(req),
    )
    out_specs = (P(req, seq, "cfg"), P(req), P(req))
    return jax.shard_map(
        per_device, mesh=split_mesh, in_specs=in_specs, out_specs=out_specs, check_vma=False
    )
```

```python
import jax
import jax.numpy as jnp
from jax import lax
from jax.experimental import pallas as pl
from jax.experimental.pallas import tpu as pltpu
from jax.sharding import Mesh, PartitionSpec as P

HEADS = 12
HD = 64
SEQ_MINOR = 4
CORES = 2


guidance_weight = 4.0


def swapped(block, axis, apart):
    count = lax.axis_size(axis)
    route = []
    for low in range(count):
        high = low | 1 << apart
        if high != low and high < count:
            route += [(low, high), (high, low)]
    return lax.ppermute(block, axis, route)


def attention_partials_kernel(q_ref, kv_ref, mask_ref, out_ref):
    rows = q_ref.shape[0]
    lanes = 2 * HD
    lane = lax.broadcasted_iota(jnp.int32, (1, lanes), 1)
    low = lane < HD
    usable = mask_ref[...] > 0
    factor = HD ** (-0.5)
    maxes = []
    sums = []
    for pair in range(HEADS // 2):
        cols = slice(pair * lanes, (pair + 1) * lanes)
        q2 = q_ref[:, cols]
        k2 = jnp.concatenate([kv_ref[z, 0, :, cols] for z in range(kv_ref.shape[0])], axis=0)
        v2 = jnp.concatenate([kv_ref[z, 1, :, cols] for z in range(kv_ref.shape[0])], axis=0)
        outs = []
        for half in (low, jnp.logical_not(low)):
            q_half = jnp.where(half, q2, jnp.zeros_like(q2))
            logits = lax.dot_general(
                q_half, k2, (((1,), (1,)), ((), ())), preferred_element_type=jnp.float32
            ) * factor
            part_max = jnp.max(jnp.where(usable, logits, -1e30), axis=1, keepdims=True)
            weights = jnp.where(usable, jnp.exp(logits - part_max), 0.0)
            sums.append(jnp.sum(weights, axis=1, keepdims=True))
            maxes.append(part_max)
            outs.append(
                jnp.dot(weights.astype(jnp.bfloat16), v2, preferred_element_type=jnp.float32)
            )
        out_ref[:, cols] = jnp.where(low, outs[0], outs[1])
    width = HEADS * HD
    out_ref[:, width : width + HEADS] = jnp.concatenate(maxes, axis=1)
    out_ref[:, width + HEADS : width + 2 * HEADS] = jnp.concatenate(sums, axis=1)

def attention_partials(q, kv, mask):
    rows = q.shape[0]
    width = HEADS * HD
    return pl.pallas_call(
        attention_partials_kernel,
        out_shape=jax.ShapeDtypeStruct((rows, width + 2 * HEADS), jnp.float32),
        in_specs=[pl.BlockSpec(memory_space=pltpu.VMEM)] * 3,
        out_specs=pl.BlockSpec(memory_space=pltpu.VMEM),
        cost_estimate=pl.CostEstimate(
            flops=8 * rows * kv.shape[0] * kv.shape[2] * width,
            transcendentals=2 * rows * kv.shape[0] * kv.shape[2] * HEADS,
            bytes_accessed=q.size * 2 + kv.size * 2 + rows * (width + 2 * HEADS) * 4,
        ),
    )(q, kv, mask)


def modulate_rows(hidden, shift_row, scale_row):
    row_mean = jnp.mean(hidden, axis=1, keepdims=True)
    centered = hidden - row_mean
    row_var = jnp.mean(centered * centered, axis=1, keepdims=True)
    return (
        centered * lax.rsqrt(row_var + 1e-06) * (1.0 + scale_row[None, :]) + shift_row[None, :]
    ).astype(jnp.bfloat16)


def per_device(
    query,
    key_value,
    residual_in,
    text_len,
    attn_gate,
    mlp_shift,
    mlp_scale,
    mlp_gate,
    shift,
    scale,
    w_proj,
    w_up,
    w_down,
    w_out,
    latent,
    step_size,
):
    img_dev = query.shape[2]
    rows_dev = key_value.shape[3]
    txt_dev = rows_dev - img_dev
    length = text_len[0, 0]
    factor = HD ** (-0.5)
    n_x = lax.axis_size("sx")
    x_index = lax.axis_index("sx")
    n_z = lax.axis_size("sz")
    kv_blocks = lax.all_to_all(
        jnp.broadcast_to(key_value[:, 0, 0][None], (n_z,) + key_value[:, 0, 0].shape),
        "sz",
        0,
        0,
        tiled=True,
    )
    query_rows = lax.all_gather(query[0, 0], "sx", axis=0, tiled=True)
    up_other = lax.ppermute(w_up, "rc", [(0, 1), (1, 0)])
    down_other = lax.ppermute(w_down, "rc", [(0, 1), (1, 0)])
    query_rows, up_other, down_other = lax.optimization_barrier((query_rows, up_other, down_other))
    q_rows = query_rows.shape[0]
    piece_rows = n_z * rows_dev
    positions = jnp.arange(piece_rows, dtype=jnp.int32)
    within = positions % rows_dev
    source = (positions // rows_dev) * n_x + x_index
    text_slot = source * txt_dev + within - img_dev
    usable = ((within < img_dev) | (text_slot < length)).astype(jnp.float32)[None, :]
    width = HEADS * HD
    packed = attention_partials(
        query_rows, kv_blocks, usable
    ).reshape(n_x, img_dev, width + 2 * HEADS)
    got = lax.all_to_all(packed, "sx", 0, 0, tiled=True)
    got_out = got[:, :, :width].reshape(n_x, img_dev, HEADS, HD)
    got_max = got[:, :, width : width + HEADS]
    got_sum = got[:, :, width + HEADS :]
    row_max = jnp.max(got_max, axis=0)
    rescale = jnp.exp(got_max - row_max[None])
    numerator = jnp.sum(rescale[:, :, :, None] * got_out, axis=0)
    denominator = jnp.sum(rescale * got_sum, axis=0)
    attended = (numerator / denominator[:, :, None]).reshape(img_dev, width).astype(jnp.bfloat16)
    projected = jnp.dot(
        attended,
        lax.all_gather(w_proj, ("ry", "rc"), axis=1, tiled=True),
        preferred_element_type=jnp.float32,
    )
    hidden = residual_in[0, 0].astype(jnp.float32) + attn_gate[0, 0][None, :] * projected
    mlp_in = modulate_rows(hidden, mlp_shift[0, 0], mlp_scale[0, 0])
    n_y = lax.axis_size("ry")
    pair = [(0, 1), (1, 0)]
    line_in = lax.all_gather(mlp_in, "ry", axis=0, tiled=True)
    inner_own = jax.nn.gelu(
        jnp.dot(line_in, w_up, preferred_element_type=jnp.float32), approximate=True
    ).astype(jnp.bfloat16)
    inner_other = jax.nn.gelu(
        jnp.dot(line_in, up_other, preferred_element_type=jnp.float32), approximate=True
    ).astype(jnp.bfloat16)
    mlp_parts = (
        (
            jnp.dot(inner_own, w_down, preferred_element_type=jnp.float32)
            + jnp.dot(inner_other, down_other, preferred_element_type=jnp.float32)
        )
        .astype(jnp.bfloat16)
        .reshape(n_y, img_dev, w_down.shape[1])
    )
    mlp_out = jnp.sum(
        lax.all_to_all(mlp_parts, "ry", 0, 0, tiled=True).astype(jnp.float32), axis=0
    )
    hidden_two = hidden + mlp_gate[0, 0][None, :] * mlp_out
    modulated = modulate_rows(hidden_two, shift[0, 0], scale[0, 0])
    velocity = jnp.dot(modulated, w_out, preferred_element_type=jnp.float32)
    half_width = velocity.shape[1] // lax.axis_size("cfg")
    side_index = lax.axis_index("cfg")
    received = swapped(velocity, "cfg", 0)
    is_cond = side_index == 0
    cond_part = jnp.where(is_cond, velocity, received)
    uncond = jnp.where(is_cond, received, velocity)
    guided_full = uncond + guidance_weight * (cond_part - uncond)
    partials = jnp.stack([jnp.sum(guided_full * guided_full), jnp.max(jnp.abs(guided_full))])
    n_seq = lax.axis_size(("sz", "sx"))
    gathered = lax.all_to_all(
        jnp.broadcast_to(partials[None], (n_seq, 2)), ("sz", "sx"), 0, 0, tiled=True
    )
    guided_total = jnp.sum(gathered[:, 0])
    peak_value = jnp.max(gathered[:, 1])
    entries = img_dev * n_seq * velocity.shape[1]
    guided_norm = jnp.sqrt(guided_total / entries + 1e-06)
    guided = lax.dynamic_slice_in_dim(guided_full, side_index * half_width, half_width, 1)
    latent_next = latent + step_size[0] * guided[None, :, :]
    return (latent_next, jnp.reshape(guided_norm, (1,)), jnp.reshape(peak_value, (1,)))


def solution(mesh):
    n_seq = mesh.shape["seq"]
    n_req = mesh.shape["req"]
    n_x = SEQ_MINOR if n_seq % SEQ_MINOR == 0 else 1
    n_core = CORES if n_req % CORES == 0 else 1
    split_mesh = Mesh(
        mesh.devices.reshape(mesh.shape["cfg"], n_req // n_core, n_core, n_seq // n_x, n_x),
        ("cfg", "ry", "rc", "sz", "sx"),
    )
    req = ("ry", "rc")
    seq = ("sz", "sx")
    in_specs = (
        P("cfg", req, seq, None),
        P(None, "cfg", req, seq, None),
        P("cfg", req, seq, None),
        P("cfg", req),
        P("cfg", req, None),
        P("cfg", req, None),
        P("cfg", req, None),
        P("cfg", req, None),
        P("cfg", req, None),
        P("cfg", req, None),
        P(None, req),
        P(None, req),
        P(req, None),
        P(),
        P(req, seq, "cfg"),
        P(req),
    )
    out_specs = (P(req, seq, "cfg"), P(req), P(req))
    return jax.shard_map(
        per_device, mesh=split_mesh, in_specs=in_specs, out_specs=out_specs, check_vma=False
    )
```
